256 devices in a mesh: section: 8 (over z), joint: 32 (over y, x, core).
Axes of the slice: x: 4, y: 4, z: 8, core: 2. Of those that a mesh axis runs over, the one named last changes fastest.
Arguments:
- encoder_rows: bfloat16 [32, 1024, 1536], P('joint', 'section'), may hold values from -6 to 6
- up_weight: bfloat16 [1536, 3072], P(None, 'section'), may hold values from -0.15625 to 0.15625
- down_weight: bfloat16 [3072, 1536], P('section'), may hold values from -0.109375 to 0.109375
- encoder_proj: bfloat16 [1536, 640], replicated, may hold values from -0.15625 to 0.15625
- embedding: bfloat16 [4096, 640], P('joint'), may hold values from -6 to 6
- conv_taps: float32 [2, 640], replicated, may hold values from -3 to 3
- decoder_proj: bfloat16 [640, 640], replicated, may hold values from -0.25 to 0.25
- output_proj: bfloat16 [640, 4096], replicated, may hold values from -0.5 to 0.5
- output_bias: float32 [4096], replicated, may hold values from -6 to 6
- frame_lengths: int32 [32], replicated, may hold values from 1 to 1024, 20480 in all
- label_lengths: int32 [32], replicated, may hold values from 1 to 3, 48 in all
- label_ids: int32 [32, 3], replicated, may hold values from 1 to 4095
- owner_index: int32 [32], replicated, may hold values from 0 to 31, each once
Outputs:
- enc_grad: bfloat16 [32, 1024, 1536], P('joint', 'section')
- up_grad: float32 [1536, 3072], P('joint', 'section')
- down_grad: float32 [3072, 1536], P('section', 'joint')
- pred_grad: float32 [32, 4, 640], P('joint', None, 'section')
The draws below stay inside these ranges and needn't reach their ends.
Inputs may be any that keep to these rules, and one draw needn't show every extreme that they name: `owner_index`: every joint owner receives exactly one utterance. `frame_lengths`: the longest utterance uses all 1024 frames. `label_lengths`: the longest label sequence has 3 labels. `label_ids`: never the blank token 0.
All inputs are finite; a program needn't handle non-finite values.
Results may differ from the reference program's by a relative error of at most 0.013.
Values may be sent and summed in bfloat16 or wider, within the bound.
No kernel may reach another device: no remote copies, remote signals or barrier semaphores. Data moves between devices by JAX's collectives and lax.ppermute only.
A program may use at most 128 MiB of HBM per device.

```python
import math
import jax
import jax.numpy as jnp
import numpy as np
from jax import lax

D = 1536
FF = 3072
JD = 640
PD = 640
V = 4096
ULAB = 3
TMAX = 1024
UTT = 32


def with_ends(values, rng, low, high):
    longest = values.shape.index(max(values.shape))
    spots = []
    for shift in (0, 1):
        where = [jax.random.randint(jax.random.fold_in(rng, axis), (), 0, length) for axis, length in enumerate(values.shape)]
        where[longest] = (where[longest] + shift) % values.shape[longest]
        spots.append(tuple(where))
    return values.at[spots[0]].set(low).at[spots[1]].set(high)


def steps_of(stream_key, extent, shards, smallest, largest):
    loudness, own = 1.0, jax.random.fold_in(stream_key, 6)
    for dim, shards_of in shards:
        steps = jnp.exp(jax.random.uniform(jax.random.fold_in(own, dim), (shards_of,), jnp.float32, smallest / len(shards), largest / len(shards)))
        loudness = loudness * jnp.repeat(steps, extent[dim] // shards_of).reshape([-1 if axis == dim else 1 for axis in range(len(extent))])
    return loudness


def split_up(count, total, bound, lean):
    weights = [(1 << 20) // math.isqrt(rank ** lean) + 1 for rank in range(2, count + 1)]
    surplus, given = total - bound - (count - 1), [1] * (count - 1)
    while surplus > 0:
        movable = [i for i in range(count - 1) if given[i] < bound]
        mass, budget = sum([weights[i] for i in movable]), surplus
        for i in movable:
            more = min(bound - given[i], max(1, budget * weights[i] // mass), surplus)
            given[i] = given[i] + more
            surplus = surplus - more
    return np.array([bound] + given)


def uneven(stream_key, number_of, total, most, skew):
    if number_of == 2:
        one = jax.random.randint(stream_key, (), max(1, total - most), min(most, total - 1) + 1)
        return jnp.stack([one, total - one])
    tallies = jnp.asarray(split_up(number_of, total, most, skew), jnp.int32)
    twos = (number_of - 1) // 2
    donor, sink = tallies[1:1 + 2 * twos:2], tallies[2:2 + 2 * twos:2]
    margin = jnp.minimum(donor - 1, most - sink)
    passed = jax.random.randint(jax.random.fold_in(stream_key, 1), (twos,), 0, 1 << 20) % (margin + 1)
    tallies = tallies.at[1:1 + 2 * twos:2].set(donor - passed).at[2:2 + 2 * twos:2].set(sink + passed)
    return tallies[jax.random.permutation(jax.random.fold_in(stream_key, 2), number_of)]


def scatter_about(key, extent, deviation, most, shards=(), held_as=jnp.bfloat16):
    values = jax.random.normal(key, extent, jnp.float32) * deviation
    if len(shards) > 0:
        values = steps_of(key, extent, shards, -0.22, 0.18) * values
    return jnp.clip(values, min=-most, max=most).astype(held_as)


def setup_inputs(seed: int = 0) -> dict:
    splits = jax.random.split(jax.random.key(seed), 14)
    return {
        "encoder_rows": scatter_about(splits[0], (UTT, TMAX, D), 1.0, 6.0, ((0, 32), (1, 8))),
        "up_weight": scatter_about(splits[1], (D, FF), D ** -0.5, 0.15625, ((1, 8),)),
        "down_weight": scatter_about(splits[2], (FF, D), FF ** -0.5, 0.109375, ((0, 8),)),
        "encoder_proj": scatter_about(splits[3], (D, JD), D ** -0.5, 0.15625),
        "embedding": scatter_about(splits[4], (V, PD), 1.0, 6.0, ((0, 32),)),
        "conv_taps": scatter_about(splits[5], (2, PD), 1.0, 3.0, (), jnp.float32),
        "decoder_proj": scatter_about(splits[6], (PD, JD), PD ** -0.5, 0.25),
        "output_proj": scatter_about(splits[7], (JD, V), (JD // 4) ** -0.5, 0.5),
        "output_bias": scatter_about(splits[8], (V,), 1.0, 6.0, (), jnp.float32),
        "frame_lengths": uneven(splits[9], UTT, UTT * TMAX * 5 // 8, TMAX, 2).astype(jnp.int32),
        "label_lengths": uneven(splits[10], UTT, UTT * ULAB // 2, ULAB, 2).astype(jnp.int32),
        "label_ids": with_ends(jax.random.randint(splits[11], (UTT, ULAB), 1, V), jax.random.fold_in(splits[11], 1), 1, V - 1).astype(jnp.int32),
        "owner_index": jax.random.permutation(splits[12], UTT).astype(jnp.int32),
    }


NEG_BIG = -1000000000.0

def layer_norm(values):
    average = lax.optimization_barrier(jnp.mean(values, axis=-1, keepdims=True))
    centered = values - average
    variance = lax.optimization_barrier(jnp.mean(centered * centered, axis=-1, keepdims=True))
    inv_scale = lax.rsqrt(variance + 1e-05)
    return (centered * inv_scale, inv_scale)

def lower_paths(label_row):
    partial_sums = jnp.concatenate([jnp.zeros((1,), jnp.float32), jnp.cumsum(label_row)])
    places = partial_sums.shape[0]
    row_ids = lax.broadcasted_iota(jnp.int32, (places, places), 0)
    col_ids = lax.broadcasted_iota(jnp.int32, (places, places), 1)
    return jnp.where(col_ids <= row_ids, partial_sums[:, None] - partial_sums[None, :], NEG_BIG)

def advance(vector, blank_row, label_row, active):
    moved = blank_row + jax.nn.logsumexp(lower_paths(label_row) + vector[None, :], axis=1)
    return jnp.where(active, moved, vector)

def run_block(vector, blank_score, label_score, active):

    def one_frame(carried, inputs):
        blank_row, label_row, live_flag = inputs
        return (advance(carried, blank_row, label_row, live_flag), None)
    return lax.scan(one_frame, vector, (blank_score, label_score, active))[0]

def joint_forward(frame_part, pred_here, label_row_ids, output_proj, output_bias):
    joined = jnp.tanh(frame_part.astype(jnp.float32)[:, None, :] + pred_here[None, :, :]).astype(jnp.bfloat16)
    frames_here, places, joint_width = joined.shape
    logits = jnp.dot(joined.reshape(frames_here * places, joint_width), output_proj, preferred_element_type=jnp.float32) + output_bias
    logits = logits.reshape(frames_here, places, -1)
    exponent = jnp.exp(logits)
    denominator = lax.optimization_barrier(jnp.sum(exponent, axis=-1, keepdims=True))
    log_total = jnp.log(denominator)[:, :, 0]
    blank_score = logits[:, :, 0] - log_total
    index_grid = jnp.broadcast_to(label_row_ids[None, :, None], (frames_here, places - 1, 1))
    picked = jnp.take_along_axis(logits[:, :-1, :], index_grid, axis=2)[:, :, 0]
    label_score = picked - log_total[:, :-1]
    posterior = exponent / denominator
    return (joined, posterior, blank_score, label_score)

def joint_backward(blank_grad, label_grad, label_row_ids, joined, posterior, output_proj):
    frames_here, places, vocab_size = posterior.shape
    weight_sum = blank_grad + jnp.pad(label_grad, ((0, 0), (0, 1)))
    logit_grad = -posterior * weight_sum[:, :, None]
    logit_grad = logit_grad.at[:, :, 0].add(blank_grad)
    frame_ids = lax.broadcasted_iota(jnp.int32, (frames_here, places - 1), 0)
    place_ids = lax.broadcasted_iota(jnp.int32, (frames_here, places - 1), 1)
    label_grid = jnp.broadcast_to(label_row_ids[None, :], (frames_here, places - 1))
    logit_grad = logit_grad.at[frame_ids, place_ids, label_grid].add(label_grad)
    logit_grad = logit_grad.astype(jnp.bfloat16).reshape(frames_here * places, vocab_size)
    joined_grad = lax.dot_general(logit_grad, output_proj, (((1,), (1,)), ((), ())), preferred_element_type=jnp.float32)
    joined_vals = joined.astype(jnp.float32).reshape(frames_here * places, -1)
    inner_grad = (joined_grad * (1.0 - joined_vals * joined_vals)).reshape(frames_here, places, -1)
    frame_part_grad = lax.optimization_barrier(jnp.sum(inner_grad, axis=1)).astype(jnp.bfloat16)
    pred_part_grad = lax.optimization_barrier(jnp.sum(inner_grad, axis=0))
    return (frame_part_grad, pred_part_grad)

def reference(encoder_rows, up_weight, down_weight, encoder_proj, embedding, conv_taps, decoder_proj, output_proj, output_bias, frame_lengths, label_lengths, label_ids, owner_index):
    utterances, frames_all, model_width = encoder_rows.shape
    flat_rows = encoder_rows.reshape(utterances * frames_all, model_width).astype(jnp.float32)
    normed_in = layer_norm(flat_rows)[0].astype(jnp.bfloat16)
    pre_hidden = jnp.dot(normed_in, up_weight, preferred_element_type=jnp.float32)
    hidden = jax.nn.silu(pre_hidden).astype(jnp.bfloat16)
    encoded = flat_rows + 0.5 * jnp.dot(hidden, down_weight, preferred_element_type=jnp.float32)
    unit_rows, inv_scale = layer_norm(encoded)
    frame_part = jnp.dot(unit_rows.astype(jnp.bfloat16), encoder_proj, preferred_element_type=jnp.float32).astype(jnp.bfloat16)
    joint_width = frame_part.shape[1]
    frame_part = frame_part.reshape(utterances, frames_all, joint_width)
    context = jnp.concatenate([jnp.zeros((utterances, 1), jnp.int32), label_ids], axis=1)
    looked = embedding[context].astype(jnp.float32)
    previous = jnp.concatenate([looked[:, :1], looked[:, :-1]], axis=1)
    pred_act = jnp.maximum(conv_taps[0] * previous + conv_taps[1] * looked, 0.0).astype(jnp.bfloat16)
    places = context.shape[1]
    pred_rows = jnp.dot(pred_act.reshape(utterances * places, -1), decoder_proj, preferred_element_type=jnp.float32).reshape(utterances, places, -1)
    frame_iota = jnp.arange(frames_all, dtype=jnp.int32)
    place_iota = jnp.arange(places, dtype=jnp.int32)
    start_vec = jnp.where(place_iota == 0, 0.0, NEG_BIG)

    def per_utterance(inputs):
        frame_here, pred_here, label_here, frames_used, labels_used = inputs
        joined, posterior, blank_score, label_score = joint_forward(frame_here, pred_here, label_here, output_proj, output_bias)
        active = frame_iota < frames_used

        def neg_logprob(blank_in, label_in):
            final_vec = run_block(start_vec, blank_in, label_in, active)
            return -jnp.sum(jnp.where(place_iota == labels_used, final_vec, 0.0))
        loss_value, pullback = jax.vjp(neg_logprob, blank_score, label_score)
        blank_grad, label_grad = pullback(jnp.ones_like(loss_value))
        return joint_backward(blank_grad, label_grad, label_here, joined, posterior, output_proj)
    part_grads, pred_grads = lax.map(per_utterance, (frame_part, pred_rows, label_ids, frame_lengths, label_lengths))
    grad_parts = part_grads.reshape(utterances * frames_all, joint_width)
    unit_grad = lax.dot_general(grad_parts, encoder_proj, (((1,), (1,)), ((), ())), preferred_element_type=jnp.float32)
    first_mean = lax.optimization_barrier(jnp.mean(unit_grad, axis=-1, keepdims=True))
    second_mean = lax.optimization_barrier(jnp.mean(unit_grad * unit_rows, axis=-1, keepdims=True))
    grad_flat = (inv_scale * (unit_grad - first_mean - unit_rows * second_mean)).astype(jnp.bfloat16)
    hidden_grad = 0.5 * lax.dot_general(grad_flat, down_weight, (((1,), (1,)), ((), ())), preferred_element_type=jnp.float32)
    gate_sigmoid = jax.nn.sigmoid(pre_hidden)
    pre_grad = (hidden_grad * gate_sigmoid * (1.0 + pre_hidden * (1.0 - gate_sigmoid))).astype(jnp.bfloat16)
    up_grad = lax.dot_general(normed_in, pre_grad, (((0,), (0,)), ((), ())), preferred_element_type=jnp.float32)
    down_grad = 0.5 * lax.dot_general(hidden, grad_flat, (((0,), (0,)), ((), ())), preferred_element_type=jnp.float32)
    enc_grad = grad_flat.reshape(utterances, frames_all, model_width)
    pred_grad = jnp.zeros_like(pred_grads).at[owner_index].set(pred_grads)
    return (enc_grad, up_grad, down_grad, pred_grad)
```

```python
import jax
import jax.numpy as jnp
from jax import lax
from jax.sharding import PartitionSpec as P

NEG_BIG = -1000000000.0


def partner_2(block, axis, bit):
    count = lax.axis_size(axis)
    route = []
    for low in range(count):
        high = low | 1 << bit
        if high != low and high < count:
            route += [(low, high), (high, low)]
    return lax.ppermute(block, axis, route)


def from_behind(value, axis, steps):
    count = lax.axis_size(axis)
    initial, last = (max(0, -steps), min(count, count - steps))
    return lax.ppermute(value, axis, [(source, source + steps) for source in range(initial, last)])


def layer_norm(values):
    average = jnp.mean(values, axis=-1, keepdims=True)
    centered = values - average
    variance = jnp.mean(centered * centered, axis=-1, keepdims=True)
    inv_scale = lax.rsqrt(variance + 1e-05)
    return (centered * inv_scale, inv_scale)


def lower_paths(label_row):
    partial_sums = jnp.concatenate([jnp.zeros((1,), jnp.float32), jnp.cumsum(label_row)])
    places = partial_sums.shape[0]
    row_ids = lax.broadcasted_iota(jnp.int32, (places, places), 0)
    col_ids = lax.broadcasted_iota(jnp.int32, (places, places), 1)
    return jnp.where(col_ids <= row_ids, partial_sums[:, None] - partial_sums[None, :], NEG_BIG)


def advance(vector, blank_row, label_row, active):
    moved = blank_row + jax.nn.logsumexp(lower_paths(label_row) + vector[None, :], axis=1)
    return jnp.where(active, moved, vector)


def run_block(vector, blank_score, label_score, active):

    def run_one_frame(carried, inputs):
        blank_row, label_row, live_flag = inputs
        return (advance(carried, blank_row, label_row, live_flag), None)

    return lax.scan(run_one_frame, vector, (blank_score, label_score, active))[0]


def block_matrix(blank_score, label_score, active):
    places = blank_score.shape[1]
    row_ids = lax.broadcasted_iota(jnp.int32, (places, places), 0)
    col_ids = lax.broadcasted_iota(jnp.int32, (places, places), 1)
    identity_map = jnp.where(row_ids == col_ids, 0.0, NEG_BIG)

    def block_one_frame(carried, inputs):
        blank_row, label_row, live_flag = inputs
        moved = blank_row[:, None] + jax.nn.logsumexp(
            lower_paths(label_row)[:, :, None] + carried[None, :, :], axis=1
        )
        return (jnp.where(live_flag, moved, carried), None)

    return lax.scan(block_one_frame, identity_map, (blank_score, label_score, active))[0]


def log_apply(transfer, vector):
    return jax.nn.logsumexp(transfer + vector[None, :], axis=1)


def log_apply_back(transfer, vector):
    return jax.nn.logsumexp(transfer + vector[:, None], axis=0)


def log_combine(earlier, later):
    terms = later[..., :, :, None] + earlier[..., None, :, :]
    return jax.nn.logsumexp(terms, axis=-2)


def prefix_products(mats):
    count = mats.shape[-3]
    index = lax.broadcasted_iota(jnp.int32, (count, 1, 1), 0)
    step = 1
    while step < count:
        shifted = jnp.concatenate([mats[..., :step, :, :], mats[..., :-step, :, :]], axis=-3)
        mats = jnp.where(index >= step, log_combine(shifted, mats), mats)
        step *= 2
    return mats


def both_products(mats):
    backward = jnp.swapaxes(jnp.flip(mats, axis=0), -1, -2)
    scanned = prefix_products(jnp.stack([mats, backward]))
    return scanned[0], jnp.flip(scanned[1], axis=0)


def identity_of(places):
    row_ids = lax.broadcasted_iota(jnp.int32, (places, places), 0)
    col_ids = lax.broadcasted_iota(jnp.int32, (places, places), 1)
    return jnp.where(row_ids == col_ids, 0.0, NEG_BIG)


def frame_matrices(blank_score, label_score, active):
    frames, places = blank_score.shape
    partial = jnp.concatenate(
        [jnp.zeros((frames, 1), jnp.float32), jnp.cumsum(label_score, axis=1)], axis=1
    )
    row_ids = lax.broadcasted_iota(jnp.int32, (1, places, places), 1)
    col_ids = lax.broadcasted_iota(jnp.int32, (1, places, places), 2)
    moved = jnp.where(
        col_ids <= row_ids,
        blank_score[:, :, None] + partial[:, :, None] - partial[:, None, :],
        NEG_BIG,
    )
    return jnp.where(active[:, None, None], moved, identity_of(places)[None])


def ends_of(transfers, block_id, start_vec, finish_vec):
    places = start_vec.shape[0]
    forward, backward_t = both_products(transfers)
    eye = identity_of(places)[None]
    before = jnp.concatenate([eye, forward[:-1]], axis=0)[block_id]
    after_t = jnp.concatenate([backward_t[1:], eye], axis=0)[block_id]
    incoming = jax.nn.logsumexp(before + start_vec[None, :], axis=1)
    leaving = jax.nn.logsumexp(after_t + finish_vec[None, :], axis=1)
    return incoming, leaving


def frame_grads(mats, forward, backward_t, incoming, leaving, active):
    places = mats.shape[-1]
    reached = jax.nn.logsumexp(forward + incoming[None, None, :], axis=2)
    alpha = jnp.concatenate([incoming[None], reached[:-1]], axis=0)
    remaining = jax.nn.logsumexp(backward_t + leaving[None, None, :], axis=2)
    beta = jnp.concatenate([remaining[1:], leaving[None]], axis=0)
    joint = alpha[:, None, :] + mats + beta[:, :, None]
    frames = joint.shape[0]
    flat = jax.nn.softmax(joint.reshape(frames, places * places), axis=1)
    weights = jnp.where(active[:, None, None], flat.reshape(frames, places, places), 0.0)
    blank_grad = -jnp.sum(weights, axis=2)
    slot = lax.broadcasted_iota(jnp.int32, (places - 1, places, places), 0)
    row_ids = lax.broadcasted_iota(jnp.int32, (places - 1, places, places), 1)
    col_ids = lax.broadcasted_iota(jnp.int32, (places - 1, places, places), 2)
    cover = ((col_ids <= slot) & (slot < row_ids)).astype(jnp.float32)
    label_grad = -jnp.einsum("tkj,ikj->ti", weights, cover, precision=lax.Precision.HIGHEST)
    return blank_grad, label_grad


def joint_forward(frame_part, pred_here, label_row_ids, output_proj, output_bias):
    joined = jnp.tanh(frame_part.astype(jnp.float32)[:, None, :] + pred_here[None, :, :]).astype(
        jnp.bfloat16
    )
    frames_here, places, joint_width = joined.shape
    logits = (
        jnp.dot(
            joined.reshape(frames_here * places, joint_width),
            output_proj,
            preferred_element_type=jnp.float32,
        )
        + output_bias
    )
    logits = logits.reshape(frames_here, places, -1)
    exponent = jnp.exp(logits)
    denominator = jnp.sum(exponent, axis=-1, keepdims=True)
    log_total = jnp.log(denominator)[:, :, 0]
    blank_score = logits[:, :, 0] - log_total
    index_grid = jnp.broadcast_to(label_row_ids[None, :, None], (frames_here, places - 1, 1))
    picked = jnp.take_along_axis(logits[:, :-1, :], index_grid, axis=2)[:, :, 0]
    label_score = picked - log_total[:, :-1]
    posterior = exponent / denominator
    return (joined, posterior, blank_score, label_score)


def joint_backward(blank_grad, label_grad, label_row_ids, joined, posterior, output_proj):
    frames_here, places, vocab_size = posterior.shape
    label_full = jnp.pad(label_grad, ((0, 0), (0, 1)))
    weight_sum = blank_grad + label_full
    token_full = jnp.concatenate([label_row_ids, jnp.full((1,), -1, jnp.int32)])
    vocab_iota = lax.broadcasted_iota(jnp.int32, (1, 1, vocab_size), 2)
    blank_term = jnp.where(vocab_iota == 0, blank_grad[:, :, None], 0.0)
    label_term = jnp.where(vocab_iota == token_full[None, :, None], label_full[:, :, None], 0.0)
    logit_grad = -posterior * weight_sum[:, :, None] + blank_term + label_term
    logit_grad = logit_grad.astype(jnp.bfloat16).reshape(frames_here * places, vocab_size)
    joined_grad = lax.dot_general(
        logit_grad, output_proj, (((1,), (1,)), ((), ())), preferred_element_type=jnp.float32
    )
    joined_vals = joined.astype(jnp.float32).reshape(frames_here * places, -1)
    inner_grad = (joined_grad * (1.0 - joined_vals * joined_vals)).reshape(frames_here, places, -1)
    frame_part_grad = jnp.sum(inner_grad, axis=1).astype(jnp.bfloat16)
    pred_part_grad = jnp.sum(inner_grad, axis=0)
    return (frame_part_grad, pred_part_grad)


def network_sections(count):
    sections = []
    block_size = 2
    while block_size <= count:
        stride = block_size // 2
        while stride >= 1:
            sections.append((block_size, stride))
            stride = stride // 2
        block_size = block_size * 2
    return sections


def sort_section(keys, block_size, stride, device_id):
    count = keys.shape[0]
    position = jnp.arange(count, dtype=jnp.int32)
    partner = position ^ stride
    partner_keys = keys[partner]
    rising = position & block_size == 0
    lower_side = position < partner
    keep_small = lower_side == rising
    new_keys = jnp.where(
        keep_small, jnp.minimum(keys, partner_keys), jnp.maximum(keys, partner_keys)
    )
    takes = new_keys[device_id] != keys[device_id]
    return (new_keys, takes)


def route_owner(payload, keys, device_id, count):
    for block_size, stride in network_sections(count):
        keys, takes = sort_section(keys, block_size, stride, device_id)
        other = partner_2(payload, "joint", stride.bit_length() - 1)
        payload = jnp.where(takes, other, payload)
    return payload


def route_holder(payload, keys, device_id, count):
    for block_size, stride in network_sections(count):
        keys, takes = sort_section(keys, block_size, stride, device_id)
        other = partner_2(payload, "joint", stride.bit_length() - 1)
        payload = jnp.where(takes, other, payload)
    return payload


def on_device(
    encoder_rows,
    up_weight,
    down_weight,
    encoder_proj,
    embedding,
    conv_taps,
    decoder_proj,
    output_proj,
    output_bias,
    frame_lengths,
    label_lengths,
    label_ids,
    owner_index,
):
    section_count = lax.axis_size("section")
    joint_count = lax.axis_size("joint")
    section_id = lax.axis_index("section")
    joint_id = lax.axis_index("joint")
    block_len = encoder_rows.shape[1]
    utterances = label_ids.shape[0]
    places = label_ids.shape[1] + 1
    own_rows = encoder_rows[0].astype(jnp.float32)
    normed_in = layer_norm(own_rows)[0].astype(jnp.bfloat16)
    gathered = lax.all_gather(normed_in, "section", axis=0, tiled=True)
    pre_hidden = jnp.dot(gathered, up_weight, preferred_element_type=jnp.float32)
    hidden = jax.nn.silu(pre_hidden).astype(jnp.bfloat16)
    encoded = own_rows + lax.psum_scatter(
        0.5 * jnp.dot(hidden, down_weight, preferred_element_type=jnp.float32),
        "section",
        scatter_dimension=0,
        tiled=True,
    )
    unit_rows, inv_scale = layer_norm(encoded)
    frame_part = jnp.dot(
        unit_rows.astype(jnp.bfloat16), encoder_proj, preferred_element_type=jnp.float32
    ).astype(jnp.bfloat16)
    order_iota = jnp.arange(utterances, dtype=jnp.int32)
    inverse = jnp.zeros((utterances,), jnp.int32).at[owner_index].set(order_iota)
    own_utterance = inverse[joint_id]
    owner_frames = route_owner(frame_part, owner_index, joint_id, joint_count)
    context = jnp.concatenate([jnp.zeros((utterances, 1), jnp.int32), label_ids], axis=1)
    vocab_rows = embedding.shape[0]
    vocab_ids = joint_id * vocab_rows + jnp.arange(vocab_rows, dtype=jnp.int32)

    def label_term(start_row, row_count):
        number = row_count // places
        wanted = context[inverse].reshape(number * places)
        selector = (wanted[:, None] == vocab_ids[None, :]).astype(jnp.bfloat16)
        return jnp.dot(selector, embedding, preferred_element_type=jnp.float32)

    looked = lax.psum_scatter(
        label_term(jnp.int32(0), places * lax.axis_size("joint")).astype(jnp.bfloat16),
        "joint",
        scatter_dimension=0,
        tiled=True,
    ).astype(jnp.float32)
    previous = jnp.concatenate([looked[:1], looked[:-1]], axis=0)
    pred_act = jnp.maximum(conv_taps[0] * previous + conv_taps[1] * looked, 0.0).astype(
        jnp.bfloat16
    )
    pred_rows = jnp.dot(pred_act, decoder_proj, preferred_element_type=jnp.float32)
    label_here = label_ids[own_utterance]
    frames_used = frame_lengths[own_utterance]
    labels_used = label_lengths[own_utterance]
    joined, posterior, blank_score, label_score = joint_forward(
        owner_frames, pred_rows, label_here, output_proj, output_bias
    )
    frame_ids = section_id * block_len + jnp.arange(block_len, dtype=jnp.int32)
    active = frame_ids < frames_used
    mats = frame_matrices(blank_score, label_score, active)
    forward, backward_t = both_products(mats)
    transfers = lax.all_gather(forward[-1], "section", axis=0, tiled=False)
    place_iota = jnp.arange(places, dtype=jnp.int32)
    start_vec = jnp.where(place_iota == 0, 0.0, NEG_BIG)
    finish_vec = jnp.where(place_iota == labels_used, 0.0, NEG_BIG)
    incoming, leaving = ends_of(transfers, section_id, start_vec, finish_vec)
    blank_grad, label_grad = frame_grads(mats, forward, backward_t, incoming, leaving, active)
    frame_part_grad, pred_part = joint_backward(
        blank_grad, label_grad, label_here, joined, posterior, output_proj
    )
    part_grad = route_holder(frame_part_grad, inverse, joint_id, joint_count)
    unit_grad = lax.dot_general(
        part_grad, encoder_proj, (((1,), (1,)), ((), ())), preferred_element_type=jnp.float32
    )
    first_mean = jnp.mean(unit_grad, axis=-1, keepdims=True)
    second_mean = jnp.mean(unit_grad * unit_rows, axis=-1, keepdims=True)
    row_grad = (inv_scale * (unit_grad - first_mean - unit_rows * second_mean)).astype(jnp.bfloat16)
    grad_all = lax.all_gather(row_grad, "section", axis=0, tiled=True)
    hidden_grad = 0.5 * lax.dot_general(
        grad_all, down_weight, (((1,), (1,)), ((), ())), preferred_element_type=jnp.float32
    )
    gate_sigmoid = jax.nn.sigmoid(pre_hidden)
    pre_grad = (hidden_grad * gate_sigmoid * (1.0 + pre_hidden * (1.0 - gate_sigmoid))).astype(
        jnp.bfloat16
    )
    up_part = lax.dot_general(
        gathered, pre_grad, (((0,), (0,)), ((), ())), preferred_element_type=jnp.float32
    )
    down_part = 0.5 * lax.dot_general(
        hidden, grad_all, (((0,), (0,)), ((), ())), preferred_element_type=jnp.float32
    )
    up_sum, down_sum = (
        lax.psum_scatter(
            up_part.astype(jnp.bfloat16), "joint", scatter_dimension=0, tiled=True
        ).astype(jnp.float32),
        lax.psum_scatter(
            down_part.astype(jnp.bfloat16), "joint", scatter_dimension=1, tiled=True
        ).astype(jnp.float32),
    )
    pred_sum = lax.psum_scatter(pred_part[None], "section", scatter_dimension=2, tiled=True)
    return (row_grad[None], up_sum, down_sum, pred_sum)


def solution(mesh):
    return jax.shard_map(
        on_device,
        mesh=mesh,
        in_specs=(
            P("joint", "section", None),
            P(None, "section"),
            P("section", None),
            P(),
            P("joint", None),
            P(),
            P(),
            P(),
            P(),
            P(),
            P(),
            P(),
            P(),
        ),
        out_specs=(
            P("joint", "section", None),
            P("joint", "section"),
            P("section", "joint"),
            P("joint", None, "section"),
        ),
        check_vma=False,
    )
```

```python
import jax
import jax.numpy as jnp
from jax import lax
from jax.sharding import PartitionSpec as P

NEG_BIG = -1000000000.0


def partner_2(block, axis, bit):
    count = lax.axis_size(axis)
    route = []
    for low in range(count):
        high = low | 1 << bit
        if high != low and high < count:
            route += [(low, high), (high, low)]
    return lax.ppermute(block, axis, route)


def from_behind(value, axis, steps):
    count = lax.axis_size(axis)
    initial, last = (max(0, -steps), min(count, count - steps))
    return lax.ppermute(value, axis, [(source, source + steps) for source in range(initial, last)])


def layer_norm(values):
    average = jnp.mean(values, axis=-1, keepdims=True)
    centered = values - average
    variance = jnp.mean(centered * centered, axis=-1, keepdims=True)
    inv_scale = lax.rsqrt(variance + 1e-05)
    return (centered * inv_scale, inv_scale)


def lower_paths(label_row):
    partial_sums = jnp.concatenate([jnp.zeros((1,), jnp.float32), jnp.cumsum(label_row)])
    places = partial_sums.shape[0]
    row_ids = lax.broadcasted_iota(jnp.int32, (places, places), 0)
    col_ids = lax.broadcasted_iota(jnp.int32, (places, places), 1)
    return jnp.where(col_ids <= row_ids, partial_sums[:, None] - partial_sums[None, :], NEG_BIG)


def advance(vector, blank_row, label_row, active):
    moved = blank_row + jax.nn.logsumexp(lower_paths(label_row) + vector[None, :], axis=1)
    return jnp.where(active, moved, vector)


def run_block(vector, blank_score, label_score, active):

    def run_one_frame(carried, inputs):
        blank_row, label_row, live_flag = inputs
        return (advance(carried, blank_row, label_row, live_flag), None)

    return lax.scan(run_one_frame, vector, (blank_score, label_score, active))[0]


def block_matrix(blank_score, label_score, active):
    places = blank_score.shape[1]
    row_ids = lax.broadcasted_iota(jnp.int32, (places, places), 0)
    col_ids = lax.broadcasted_iota(jnp.int32, (places, places), 1)
    identity_map = jnp.where(row_ids == col_ids, 0.0, NEG_BIG)

    def block_one_frame(carried, inputs):
        blank_row, label_row, live_flag = inputs
        moved = blank_row[:, None] + jax.nn.logsumexp(
            lower_paths(label_row)[:, :, None] + carried[None, :, :], axis=1
        )
        return (jnp.where(live_flag, moved, carried), None)

    return lax.scan(block_one_frame, identity_map, (blank_score, label_score, active))[0]


def log_apply(transfer, vector):
    return jax.nn.logsumexp(transfer + vector[None, :], axis=1)


def log_apply_back(transfer, vector):
    return jax.nn.logsumexp(transfer + vector[:, None], axis=0)


def log_combine(earlier, later):
    terms = later[..., :, :, None] + earlier[..., None, :, :]
    return jax.nn.logsumexp(terms, axis=-2)


def prefix_products(mats):
    count = mats.shape[-3]
    index = lax.broadcasted_iota(jnp.int32, (count, 1, 1), 0)
    step = 1
    while step < count:
        shifted = jnp.concatenate([mats[..., :step, :, :], mats[..., :-step, :, :]], axis=-3)
        mats = jnp.where(index >= step, log_combine(shifted, mats), mats)
        step *= 2
    return mats


def both_products(mats):
    backward = jnp.swapaxes(jnp.flip(mats, axis=0), -1, -2)
    scanned = prefix_products(jnp.stack([mats, backward]))
    return scanned[0], jnp.flip(scanned[1], axis=0)


def identity_of(places):
    row_ids = lax.broadcasted_iota(jnp.int32, (places, places), 0)
    col_ids = lax.broadcasted_iota(jnp.int32, (places, places), 1)
    return jnp.where(row_ids == col_ids, 0.0, NEG_BIG)


def frame_matrices(blank_score, label_score, active):
    frames, places = blank_score.shape
    partial = jnp.concatenate(
        [jnp.zeros((frames, 1), jnp.float32), jnp.cumsum(label_score, axis=1)], axis=1
    )
    row_ids = lax.broadcasted_iota(jnp.int32, (1, places, places), 1)
    col_ids = lax.broadcasted_iota(jnp.int32, (1, places, places), 2)
    moved = jnp.where(
        col_ids <= row_ids,
        blank_score[:, :, None] + partial[:, :, None] - partial[:, None, :],
        NEG_BIG,
    )
    return jnp.where(active[:, None, None], moved, identity_of(places)[None])


def ends_of(transfers, block_id, start_vec, finish_vec):
    places = start_vec.shape[0]
    forward, backward_t = both_products(transfers)
    eye = identity_of(places)[None]
    before = jnp.concatenate([eye, forward[:-1]], axis=0)[block_id]
    after_t = jnp.concatenate([backward_t[1:], eye], axis=0)[block_id]
    incoming = jax.nn.logsumexp(before + start_vec[None, :], axis=1)
    leaving = jax.nn.logsumexp(after_t + finish_vec[None, :], axis=1)
    return incoming, leaving


def frame_grads(mats, forward, backward_t, incoming, leaving, active):
    places = mats.shape[-1]
    reached = jax.nn.logsumexp(forward + incoming[None, None, :], axis=2)
    alpha = jnp.concatenate([incoming[None], reached[:-1]], axis=0)
    remaining = jax.nn.logsumexp(backward_t + leaving[None, None, :], axis=2)
    beta = jnp.concatenate([remaining[1:], leaving[None]], axis=0)
    joint = alpha[:, None, :] + mats + beta[:, :, None]
    frames = joint.shape[0]
    flat = jax.nn.softmax(joint.reshape(frames, places * places), axis=1)
    weights = jnp.where(active[:, None, None], flat.reshape(frames, places, places), 0.0)
    blank_grad = -jnp.sum(weights, axis=2)
    slot = lax.broadcasted_iota(jnp.int32, (places - 1, places, places), 0)
    row_ids = lax.broadcasted_iota(jnp.int32, (places - 1, places, places), 1)
    col_ids = lax.broadcasted_iota(jnp.int32, (places - 1, places, places), 2)
    cover = ((col_ids <= slot) & (slot < row_ids)).astype(jnp.float32)
    label_grad = -jnp.einsum("tkj,ikj->ti", weights, cover, precision=lax.Precision.HIGHEST)
    return blank_grad, label_grad


def joint_forward(frame_part, pred_here, label_row_ids, output_proj, output_bias):
    joined = jnp.tanh(frame_part.astype(jnp.float32)[:, None, :] + pred_here[None, :, :]).astype(
        jnp.bfloat16
    )
    frames_here, places, joint_width = joined.shape
    logits = (
        jnp.dot(
            joined.reshape(frames_here * places, joint_width),
            output_proj,
            preferred_element_type=jnp.float32,
        )
        + output_bias
    )
    logits = logits.reshape(frames_here, places, -1)
    exponent = jnp.exp(logits)
    denominator = jnp.sum(exponent, axis=-1, keepdims=True)
    log_total = jnp.log(denominator)[:, :, 0]
    blank_score = logits[:, :, 0] - log_total
    index_grid = jnp.broadcast_to(label_row_ids[None, :, None], (frames_here, places - 1, 1))
    picked = jnp.take_along_axis(logits[:, :-1, :], index_grid, axis=2)[:, :, 0]
    label_score = picked - log_total[:, :-1]
    posterior = exponent / denominator
    return (joined, posterior, blank_score, label_score)


def joint_backward(blank_grad, label_grad, label_row_ids, joined, posterior, output_proj):
    frames_here, places, vocab_size = posterior.shape
    label_full = jnp.pad(label_grad, ((0, 0), (0, 1)))
    weight_sum = blank_grad + label_full
    token_full = jnp.concatenate([label_row_ids, jnp.full((1,), -1, jnp.int32)])
    vocab_iota = lax.broadcasted_iota(jnp.int32, (1, 1, vocab_size), 2)
    blank_term = jnp.where(vocab_iota == 0, blank_grad[:, :, None], 0.0)
    label_term = jnp.where(vocab_iota == token_full[None, :, None], label_full[:, :, None], 0.0)
    logit_grad = -posterior * weight_sum[:, :, None] + blank_term + label_term
    logit_grad = logit_grad.astype(jnp.bfloat16).reshape(frames_here * places, vocab_size)
    joined_grad = lax.dot_general(
        logit_grad, output_proj, (((1,), (1,)), ((), ())), preferred_element_type=jnp.float32
    )
    joined_vals = joined.astype(jnp.float32).reshape(frames_here * places, -1)
    inner_grad = (joined_grad * (1.0 - joined_vals * joined_vals)).reshape(frames_here, places, -1)
    frame_part_grad = jnp.sum(inner_grad, axis=1).astype(jnp.bfloat16)
    pred_part_grad = jnp.sum(inner_grad, axis=0)
    return (frame_part_grad, pred_part_grad)


def network_sections(count):
    sections = []
    block_size = 2
    while block_size <= count:
        stride = block_size // 2
        while stride >= 1:
            sections.append((block_size, stride))
            stride = stride // 2
        block_size = block_size * 2
    return sections


def sort_section(keys, block_size, stride, device_id):
    count = keys.shape[0]
    position = jnp.arange(count, dtype=jnp.int32)
    partner = position ^ stride
    partner_keys = keys[partner]
    rising = position & block_size == 0
    lower_side = position < partner
    keep_small = lower_side == rising
    new_keys = jnp.where(
        keep_small, jnp.minimum(keys, partner_keys), jnp.maximum(keys, partner_keys)
    )
    takes = new_keys[device_id] != keys[device_id]
    return (new_keys, takes)


def route_owner(payload, keys, device_id, count):
    for block_size, stride in network_sections(count):
        keys, takes = sort_section(keys, block_size, stride, device_id)
        other = partner_2(payload, "joint", stride.bit_length() - 1)
        payload = jnp.where(takes, other, payload)
    return payload


def route_holder(payload, keys, device_id, count):
    for block_size, stride in network_sections(count):
        keys, takes = sort_section(keys, block_size, stride, device_id)
        other = partner_2(payload, "joint", stride.bit_length() - 1)
        payload = jnp.where(takes, other, payload)
    return payload


def route_rows(payload, source_of, axis):
    count = lax.axis_size(axis)
    rows = payload.shape[0]
    spread = lax.all_to_all(payload, axis, 0, 0, tiled=True)
    spread = spread.reshape(count, rows // count, *payload.shape[1:])
    picked = jnp.take(spread, source_of, axis=0).reshape(payload.shape)
    return lax.all_to_all(picked, axis, 0, 0, tiled=True)


def on_device(
    encoder_rows,
    up_weight,
    down_weight,
    encoder_proj,
    embedding,
    conv_taps,
    decoder_proj,
    output_proj,
    output_bias,
    frame_lengths,
    label_lengths,
    label_ids,
    owner_index,
):
    section_count = lax.axis_size("section")
    joint_count = lax.axis_size("joint")
    section_id = lax.axis_index("section")
    joint_id = lax.axis_index("joint")
    block_len = encoder_rows.shape[1]
    utterances = label_ids.shape[0]
    places = label_ids.shape[1] + 1
    own_rows = encoder_rows[0].astype(jnp.float32)
    normed_in = layer_norm(own_rows)[0].astype(jnp.bfloat16)
    gathered = lax.all_gather(normed_in, "section", axis=0, tiled=True)
    pre_hidden = jnp.dot(gathered, up_weight, preferred_element_type=jnp.float32)
    hidden = jax.nn.silu(pre_hidden).astype(jnp.bfloat16)
    encoded = own_rows + lax.psum_scatter(
        0.5 * jnp.dot(hidden, down_weight, preferred_element_type=jnp.float32),
        "section",
        scatter_dimension=0,
        tiled=True,
    )
    unit_rows, inv_scale = layer_norm(encoded)
    frame_part = jnp.dot(
        unit_rows.astype(jnp.bfloat16), encoder_proj, preferred_element_type=jnp.float32
    ).astype(jnp.bfloat16)
    order_iota = jnp.arange(utterances, dtype=jnp.int32)
    inverse = jnp.zeros((utterances,), jnp.int32).at[owner_index].set(order_iota)
    own_utterance = inverse[joint_id]
    owner_frames = route_rows(frame_part, inverse, "joint")
    context = jnp.concatenate([jnp.zeros((utterances, 1), jnp.int32), label_ids], axis=1)
    vocab_rows = embedding.shape[0]
    vocab_ids = joint_id * vocab_rows + jnp.arange(vocab_rows, dtype=jnp.int32)

    def label_term(start_row, row_count):
        number = row_count // places
        wanted = context[inverse].reshape(number * places)
        selector = (wanted[:, None] == vocab_ids[None, :]).astype(jnp.bfloat16)
        return jnp.dot(selector, embedding, preferred_element_type=jnp.float32)

    looked = lax.psum_scatter(
        label_term(jnp.int32(0), places * lax.axis_size("joint")).astype(jnp.bfloat16),
        "joint",
        scatter_dimension=0,
        tiled=True,
    ).astype(jnp.float32)
    previous = jnp.concatenate([looked[:1], looked[:-1]], axis=0)
    pred_act = jnp.maximum(conv_taps[0] * previous + conv_taps[1] * looked, 0.0).astype(
        jnp.bfloat16
    )
    pred_rows = jnp.dot(pred_act, decoder_proj, preferred_element_type=jnp.float32)
    label_here = label_ids[own_utterance]
    frames_used = frame_lengths[own_utterance]
    labels_used = label_lengths[own_utterance]
    joined, posterior, blank_score, label_score = joint_forward(
        owner_frames, pred_rows, label_here, output_proj, output_bias
    )
    frame_ids = section_id * block_len + jnp.arange(block_len, dtype=jnp.int32)
    active = frame_ids < frames_used
    mats = frame_matrices(blank_score, label_score, active)
    forward, backward_t = both_products(mats)
    transfers = lax.all_gather(forward[-1], "section", axis=0, tiled=False)
    place_iota = jnp.arange(places, dtype=jnp.int32)
    start_vec = jnp.where(place_iota == 0, 0.0, NEG_BIG)
    finish_vec = jnp.where(place_iota == labels_used, 0.0, NEG_BIG)
    incoming, leaving = ends_of(transfers, section_id, start_vec, finish_vec)
    blank_grad, label_grad = frame_grads(mats, forward, backward_t, incoming, leaving, active)
    frame_part_grad, pred_part = joint_backward(
        blank_grad, label_grad, label_here, joined, posterior, output_proj
    )
    part_grad = route_rows(frame_part_grad, owner_index, "joint")
    unit_grad = lax.dot_general(
        part_grad, encoder_proj, (((1,), (1,)), ((), ())), preferred_element_type=jnp.float32
    )
    first_mean = jnp.mean(unit_grad, axis=-1, keepdims=True)
    second_mean = jnp.mean(unit_grad * unit_rows, axis=-1, keepdims=True)
    row_grad = (inv_scale * (unit_grad - first_mean - unit_rows * second_mean)).astype(jnp.bfloat16)
    grad_all = lax.all_gather(row_grad, "section", axis=0, tiled=True)
    hidden_grad = 0.5 * lax.dot_general(
        grad_all, down_weight, (((1,), (1,)), ((), ())), preferred_element_type=jnp.float32
    )
    gate_sigmoid = jax.nn.sigmoid(pre_hidden)
    pre_grad = (hidden_grad * gate_sigmoid * (1.0 + pre_hidden * (1.0 - gate_sigmoid))).astype(
        jnp.bfloat16
    )
    up_part = lax.dot_general(
        gathered, pre_grad, (((0,), (0,)), ((), ())), preferred_element_type=jnp.float32
    )
    down_part = 0.5 * lax.dot_general(
        hidden, grad_all, (((0,), (0,)), ((), ())), preferred_element_type=jnp.float32
    )
    weight_parts = jnp.concatenate([up_part, down_part.T], axis=1).astype(jnp.bfloat16)
    weight_sums = lax.psum_scatter(weight_parts, "joint", scatter_dimension=0, tiled=True).astype(
        jnp.float32
    )
    hidden_here = up_part.shape[1]
    up_sum = weight_sums[:, :hidden_here]
    down_sum = weight_sums[:, hidden_here:].T
    pred_sum = lax.psum_scatter(pred_part[None], "section", scatter_dimension=2, tiled=True)
    return (row_grad[None], up_sum, down_sum, pred_sum)


def solution(mesh):
    return jax.shard_map(
        on_device,
        mesh=mesh,
        in_specs=(
            P("joint", "section", None),
            P(None, "section"),
            P("section", None),
            P(),
            P("joint", None),
            P(),
            P(),
            P(),
            P(),
            P(),
            P(),
            P(),
            P(),
        ),
        out_specs=(
            P("joint", "section", None),
            P("joint", "section"),
            P("section", "joint"),
            P("joint", None, "section"),
        ),
        check_vma=False,
    )
```

```python
import jax
import jax.numpy as jnp
from jax import lax
from jax.sharding import PartitionSpec as P

NEG_BIG = -1000000000.0


def partner_2(block, axis, bit):
    count = lax.axis_size(axis)
    route = []
    for low in range(count):
        high = low | 1 << bit
        if high != low and high < count:
            route += [(low, high), (high, low)]
    return lax.ppermute(block, axis, route)


def from_behind(value, axis, steps):
    count = lax.axis_size(axis)
    initial, last = (max(0, -steps), min(count, count - steps))
    return lax.ppermute(value, axis, [(source, source + steps) for source in range(initial, last)])


def layer_norm(values):
    average = jnp.mean(values, axis=-1, keepdims=True)
    centered = values - average
    variance = jnp.mean(centered * centered, axis=-1, keepdims=True)
    inv_scale = lax.rsqrt(variance + 1e-05)
    return (centered * inv_scale, inv_scale)


def lower_paths(label_row):
    partial_sums = jnp.concatenate([jnp.zeros((1,), jnp.float32), jnp.cumsum(label_row)])
    places = partial_sums.shape[0]
    row_ids = lax.broadcasted_iota(jnp.int32, (places, places), 0)
    col_ids = lax.broadcasted_iota(jnp.int32, (places, places), 1)
    return jnp.where(col_ids <= row_ids, partial_sums[:, None] - partial_sums[None, :], NEG_BIG)


def advance(vector, blank_row, label_row, active):
    moved = blank_row + jax.nn.logsumexp(lower_paths(label_row) + vector[None, :], axis=1)
    return jnp.where(active, moved, vector)


def run_block(vector, blank_score, label_score, active):

    def run_one_frame(carried, inputs):
        blank_row, label_row, live_flag = inputs
        return (advance(carried, blank_row, label_row, live_flag), None)

    return lax.scan(run_one_frame, vector, (blank_score, label_score, active))[0]


def block_matrix(blank_score, label_score, active):
    places = blank_score.shape[1]
    row_ids = lax.broadcasted_iota(jnp.int32, (places, places), 0)
    col_ids = lax.broadcasted_iota(jnp.int32, (places, places), 1)
    identity_map = jnp.where(row_ids == col_ids, 0.0, NEG_BIG)

    def block_one_frame(carried, inputs):
        blank_row, label_row, live_flag = inputs
        moved = blank_row[:, None] + jax.nn.logsumexp(
            lower_paths(label_row)[:, :, None] + carried[None, :, :], axis=1
        )
        return (jnp.where(live_flag, moved, carried), None)

    return lax.scan(block_one_frame, identity_map, (blank_score, label_score, active))[0]


def log_apply(transfer, vector):
    return jax.nn.logsumexp(transfer + vector[None, :], axis=1)


def log_apply_back(transfer, vector):
    return jax.nn.logsumexp(transfer + vector[:, None], axis=0)


def log_combine(earlier, later):
    terms = later[..., :, :, None] + earlier[..., None, :, :]
    return jax.nn.logsumexp(terms, axis=-2)


def prefix_products(mats):
    count = mats.shape[-3]
    index = lax.broadcasted_iota(jnp.int32, (count, 1, 1), 0)
    step = 1
    while step < count:
        shifted = jnp.concatenate([mats[..., :step, :, :], mats[..., :-step, :, :]], axis=-3)
        mats = jnp.where(index >= step, log_combine(shifted, mats), mats)
        step *= 2
    return mats


def both_products(mats):
    backward = jnp.swapaxes(jnp.flip(mats, axis=0), -1, -2)
    scanned = prefix_products(jnp.stack([mats, backward]))
    return scanned[0], jnp.flip(scanned[1], axis=0)


def identity_of(places):
    row_ids = lax.broadcasted_iota(jnp.int32, (places, places), 0)
    col_ids = lax.broadcasted_iota(jnp.int32, (places, places), 1)
    return jnp.where(row_ids == col_ids, 0.0, NEG_BIG)


def frame_matrices(blank_score, label_score, active):
    frames, places = blank_score.shape
    partial = jnp.concatenate(
        [jnp.zeros((frames, 1), jnp.float32), jnp.cumsum(label_score, axis=1)], axis=1
    )
    row_ids = lax.broadcasted_iota(jnp.int32, (1, places, places), 1)
    col_ids = lax.broadcasted_iota(jnp.int32, (1, places, places), 2)
    moved = jnp.where(
        col_ids <= row_ids,
        blank_score[:, :, None] + partial[:, :, None] - partial[:, None, :],
        NEG_BIG,
    )
    return jnp.where(active[:, None, None], moved, identity_of(places)[None])


def ends_of(transfers, block_id, start_vec, finish_vec):
    places = start_vec.shape[0]
    forward, backward_t = both_products(transfers)
    eye = identity_of(places)[None]
    before = jnp.concatenate([eye, forward[:-1]], axis=0)[block_id]
    after_t = jnp.concatenate([backward_t[1:], eye], axis=0)[block_id]
    incoming = jax.nn.logsumexp(before + start_vec[None, :], axis=1)
    leaving = jax.nn.logsumexp(after_t + finish_vec[None, :], axis=1)
    return incoming, leaving


def frame_grads(mats, forward, backward_t, incoming, leaving, active):
    places = mats.shape[-1]
    reached = jax.nn.logsumexp(forward + incoming[None, None, :], axis=2)
    alpha = jnp.concatenate([incoming[None], reached[:-1]], axis=0)
    remaining = jax.nn.logsumexp(backward_t + leaving[None, None, :], axis=2)
    beta = jnp.concatenate([remaining[1:], leaving[None]], axis=0)
    joint = alpha[:, None, :] + mats + beta[:, :, None]
    frames = joint.shape[0]
    flat = jax.nn.softmax(joint.reshape(frames, places * places), axis=1)
    weights = jnp.where(active[:, None, None], flat.reshape(frames, places, places), 0.0)
    blank_grad = -jnp.sum(weights, axis=2)
    slot = lax.broadcasted_iota(jnp.int32, (places - 1, places, places), 0)
    row_ids = lax.broadcasted_iota(jnp.int32, (places - 1, places, places), 1)
    col_ids = lax.broadcasted_iota(jnp.int32, (places - 1, places, places), 2)
    cover = ((col_ids <= slot) & (slot < row_ids)).astype(jnp.float32)
    label_grad = -jnp.einsum("tkj,ikj->ti", weights, cover, precision=lax.Precision.HIGHEST)
    return blank_grad, label_grad


def joint_forward(frame_part, pred_here, label_row_ids, output_proj, output_bias):
    joined = jnp.tanh(frame_part.astype(jnp.float32)[:, None, :] + pred_here[None, :, :]).astype(
        jnp.bfloat16
    )
    frames_here, places, joint_width = joined.shape
    logits = (
        jnp.dot(
            joined.reshape(frames_here * places, joint_width),
            output_proj,
            preferred_element_type=jnp.float32,
        )
        + output_bias
    )
    logits = logits.reshape(frames_here, places, -1)
    exponent = jnp.exp(logits)
    denominator = jnp.sum(exponent, axis=-1, keepdims=True)
    log_total = jnp.log(denominator)[:, :, 0]
    blank_score = logits[:, :, 0] - log_total
    index_grid = jnp.broadcast_to(label_row_ids[None, :, None], (frames_here, places - 1, 1))
    picked = jnp.take_along_axis(logits[:, :-1, :], index_grid, axis=2)[:, :, 0]
    label_score = picked - log_total[:, :-1]
    posterior = exponent / denominator
    return (joined, posterior, blank_score, label_score)


def joint_backward(blank_grad, label_grad, label_row_ids, joined, posterior, output_proj):
    frames_here, places, vocab_size = posterior.shape
    label_full = jnp.pad(label_grad, ((0, 0), (0, 1)))
    weight_sum = blank_grad + label_full
    token_full = jnp.concatenate([label_row_ids, jnp.full((1,), -1, jnp.int32)])
    vocab_iota = lax.broadcasted_iota(jnp.int32, (1, 1, vocab_size), 2)
    blank_term = jnp.where(vocab_iota == 0, blank_grad[:, :, None], 0.0)
    label_term = jnp.where(vocab_iota == token_full[None, :, None], label_full[:, :, None], 0.0)
    logit_grad = -posterior * weight_sum[:, :, None] + blank_term + label_term
    logit_grad = logit_grad.astype(jnp.bfloat16).reshape(frames_here * places, vocab_size)
    joined_grad = lax.dot_general(
        logit_grad, output_proj, (((1,), (1,)), ((), ())), preferred_element_type=jnp.float32
    )
    joined_vals = joined.astype(jnp.float32).reshape(frames_here * places, -1)
    inner_grad = (joined_grad * (1.0 - joined_vals * joined_vals)).reshape(frames_here, places, -1)
    frame_part_grad = jnp.sum(inner_grad, axis=1).astype(jnp.bfloat16)
    pred_part_grad = jnp.sum(inner_grad, axis=0)
    return (frame_part_grad, pred_part_grad)


def network_sections(count):
    sections = []
    block_size = 2
    while block_size <= count:
        stride = block_size // 2
        while stride >= 1:
            sections.append((block_size, stride))
            stride = stride // 2
        block_size = block_size * 2
    return sections


def sort_section(keys, block_size, stride, device_id):
    count = keys.shape[0]
    position = jnp.arange(count, dtype=jnp.int32)
    partner = position ^ stride
    partner_keys = keys[partner]
    rising = position & block_size == 0
    lower_side = position < partner
    keep_small = lower_side == rising
    new_keys = jnp.where(
        keep_small, jnp.minimum(keys, partner_keys), jnp.maximum(keys, partner_keys)
    )
    takes = new_keys[device_id] != keys[device_id]
    return (new_keys, takes)


def route_owner(payload, keys, device_id, count):
    for block_size, stride in network_sections(count):
        keys, takes = sort_section(keys, block_size, stride, device_id)
        other = partner_2(payload, "joint", stride.bit_length() - 1)
        payload = jnp.where(takes, other, payload)
    return payload


def route_holder(payload, keys, device_id, count):
    for block_size, stride in network_sections(count):
        keys, takes = sort_section(keys, block_size, stride, device_id)
        other = partner_2(payload, "joint", stride.bit_length() - 1)
        payload = jnp.where(takes, other, payload)
    return payload


def route_rows(payload, source_of, axis):
    count = lax.axis_size(axis)
    rows = payload.shape[0]
    spread = lax.all_to_all(payload, axis, 0, 0, tiled=True)
    spread = spread.reshape(count, rows // count, *payload.shape[1:])
    picked = jnp.take(spread, source_of, axis=0).reshape(payload.shape)
    return lax.all_to_all(picked, axis, 0, 0, tiled=True)


def on_device(
    encoder_rows,
    up_weight,
    down_weight,
    encoder_proj,
    embedding,
    conv_taps,
    decoder_proj,
    output_proj,
    output_bias,
    frame_lengths,
    label_lengths,
    label_ids,
    owner_index,
):
    section_count = lax.axis_size("section")
    joint_count = lax.axis_size("joint")
    section_id = lax.axis_index("section")
    joint_id = lax.axis_index("joint")
    block_len = encoder_rows.shape[1]
    utterances = label_ids.shape[0]
    places = label_ids.shape[1] + 1
    own_rows = encoder_rows[0].astype(jnp.float32)
    normed_in = layer_norm(own_rows)[0].astype(jnp.bfloat16)
    gathered = lax.all_gather(normed_in, "section", axis=0, tiled=True)
    pre_hidden = jnp.dot(gathered, up_weight, preferred_element_type=jnp.float32)
    hidden = jax.nn.silu(pre_hidden).astype(jnp.bfloat16)
    encoded = own_rows + lax.psum_scatter(
        0.5 * jnp.dot(hidden, down_weight, preferred_element_type=jnp.float32),
        "section",
        scatter_dimension=0,
        tiled=True,
    )
    unit_rows, inv_scale = layer_norm(encoded)
    frame_part = jnp.dot(
        unit_rows.astype(jnp.bfloat16), encoder_proj, preferred_element_type=jnp.float32
    ).astype(jnp.bfloat16)
    order_iota = jnp.arange(utterances, dtype=jnp.int32)
    inverse = jnp.zeros((utterances,), jnp.int32).at[owner_index].set(order_iota)
    own_utterance = inverse[joint_id]
    owner_frames = route_rows(frame_part, inverse, "joint")
    context = jnp.concatenate([jnp.zeros((utterances, 1), jnp.int32), label_ids], axis=1)
    vocab_rows = embedding.shape[0]
    vocab_ids = joint_id * vocab_rows + jnp.arange(vocab_rows, dtype=jnp.int32)

    def label_term(start_row, row_count):
        number = row_count // places
        wanted = context[inverse].reshape(number * places)
        selector = (wanted[:, None] == vocab_ids[None, :]).astype(jnp.bfloat16)
        return jnp.dot(selector, embedding, preferred_element_type=jnp.float32)

    looked = lax.psum_scatter(
        label_term(jnp.int32(0), places * lax.axis_size("joint")).astype(jnp.bfloat16),
        "joint",
        scatter_dimension=0,
        tiled=True,
    ).astype(jnp.float32)
    previous = jnp.concatenate([looked[:1], looked[:-1]], axis=0)
    pred_act = jnp.maximum(conv_taps[0] * previous + conv_taps[1] * looked, 0.0).astype(
        jnp.bfloat16
    )
    pred_rows = jnp.dot(pred_act, decoder_proj, preferred_element_type=jnp.float32)
    label_here = label_ids[own_utterance]
    frames_used = frame_lengths[own_utterance]
    labels_used = label_lengths[own_utterance]
    joined, posterior, blank_score, label_score = joint_forward(
        owner_frames, pred_rows, label_here, output_proj, output_bias
    )
    frame_ids = section_id * block_len + jnp.arange(block_len, dtype=jnp.int32)
    active = frame_ids < frames_used
    mats = frame_matrices(blank_score, label_score, active)
    forward, backward_t = both_products(mats)
    transfers = lax.all_to_all(
        jnp.broadcast_to(forward[-1][None], (section_count,) + forward.shape[1:]),
        "section",
        0,
        0,
        tiled=True,
    )
    place_iota = jnp.arange(places, dtype=jnp.int32)
    start_vec = jnp.where(place_iota == 0, 0.0, NEG_BIG)
    finish_vec = jnp.where(place_iota == labels_used, 0.0, NEG_BIG)
    incoming, leaving = ends_of(transfers, section_id, start_vec, finish_vec)
    blank_grad, label_grad = frame_grads(mats, forward, backward_t, incoming, leaving, active)
    frame_part_grad, pred_part = joint_backward(
        blank_grad, label_grad, label_here, joined, posterior, output_proj
    )
    part_grad = route_rows(frame_part_grad, owner_index, "joint")
    unit_grad = lax.dot_general(
        part_grad, encoder_proj, (((1,), (1,)), ((), ())), preferred_element_type=jnp.float32
    )
    first_mean = jnp.mean(unit_grad, axis=-1, keepdims=True)
    second_mean = jnp.mean(unit_grad * unit_rows, axis=-1, keepdims=True)
    row_grad = (inv_scale * (unit_grad - first_mean - unit_rows * second_mean)).astype(jnp.bfloat16)
    grad_all = lax.all_gather(row_grad, "section", axis=0, tiled=True)
    hidden_grad = 0.5 * lax.dot_general(
        grad_all, down_weight, (((1,), (1,)), ((), ())), preferred_element_type=jnp.float32
    )
    gate_sigmoid = jax.nn.sigmoid(pre_hidden)
    pre_grad = (hidden_grad * gate_sigmoid * (1.0 + pre_hidden * (1.0 - gate_sigmoid))).astype(
        jnp.bfloat16
    )
    up_part = lax.dot_general(
        gathered, pre_grad, (((0,), (0,)), ((), ())), preferred_element_type=jnp.float32
    )
    down_part = 0.5 * lax.dot_general(
        hidden, grad_all, (((0,), (0,)), ((), ())), preferred_element_type=jnp.float32
    )
    weight_parts = jnp.concatenate([up_part, down_part.T], axis=1).astype(jnp.bfloat16)
    weight_sums = lax.psum_scatter(weight_parts, "joint", scatter_dimension=0, tiled=True).astype(
        jnp.float32
    )
    hidden_here = up_part.shape[1]
    up_sum = weight_sums[:, :hidden_here]
    down_sum = weight_sums[:, hidden_here:].T
    pred_pieces = jnp.swapaxes(pred_part.reshape(places, section_count, -1), 0, 1)
    pred_sum = jnp.sum(lax.all_to_all(pred_pieces, "section", 0, 0, tiled=True), axis=0)[None]
    return (row_grad[None], up_sum, down_sum, pred_sum)


def solution(mesh):
    return jax.shard_map(
        on_device,
        mesh=mesh,
        in_specs=(
            P("joint", "section", None),
            P(None, "section"),
            P("section", None),
            P(),
            P("joint", None),
            P(),
            P(),
            P(),
            P(),
            P(),
            P(),
            P(),
            P(),
        ),
        out_specs=(
            P("joint", "section", None),
            P("joint", "section"),
            P("section", "joint"),
            P("joint", None, "section"),
        ),
        check_vma=False,
    )
```

```python
import jax
import jax.numpy as jnp
from jax import lax
from jax.sharding import PartitionSpec as P

NEG_BIG = -1000000000.0


def partner_2(block, axis, bit):
    count = lax.axis_size(axis)
    route = []
    for low in range(count):
        high = low | 1 << bit
        if high != low and high < count:
            route += [(low, high), (high, low)]
    return lax.ppermute(block, axis, route)


def from_behind(value, axis, steps):
    count = lax.axis_size(axis)
    initial, last = (max(0, -steps), min(count, count - steps))
    return lax.ppermute(value, axis, [(source, source + steps) for source in range(initial, last)])


def layer_norm(values):
    average = jnp.mean(values, axis=-1, keepdims=True)
    centered = values - average
    variance = jnp.mean(centered * centered, axis=-1, keepdims=True)
    inv_scale = lax.rsqrt(variance + 1e-05)
    return (centered * inv_scale, inv_scale)


def lower_paths(label_row):
    partial_sums = jnp.concatenate([jnp.zeros((1,), jnp.float32), jnp.cumsum(label_row)])
    places = partial_sums.shape[0]
    row_ids = lax.broadcasted_iota(jnp.int32, (places, places), 0)
    col_ids = lax.broadcasted_iota(jnp.int32, (places, places), 1)
    return jnp.where(col_ids <= row_ids, partial_sums[:, None] - partial_sums[None, :], NEG_BIG)


def advance(vector, blank_row, label_row, active):
    moved = blank_row + jax.nn.logsumexp(lower_paths(label_row) + vector[None, :], axis=1)
    return jnp.where(active, moved, vector)


def run_block(vector, blank_score, label_score, active):

    def run_one_frame(carried, inputs):
        blank_row, label_row, live_flag = inputs
        return (advance(carried, blank_row, label_row, live_flag), None)

    return lax.scan(run_one_frame, vector, (blank_score, label_score, active))[0]


def block_matrix(blank_score, label_score, active):
    places = blank_score.shape[1]
    row_ids = lax.broadcasted_iota(jnp.int32, (places, places), 0)
    col_ids = lax.broadcasted_iota(jnp.int32, (places, places), 1)
    identity_map = jnp.where(row_ids == col_ids, 0.0, NEG_BIG)

    def block_one_frame(carried, inputs):
        blank_row, label_row, live_flag = inputs
        moved = blank_row[:, None] + jax.nn.logsumexp(
            lower_paths(label_row)[:, :, None] + carried[None, :, :], axis=1
        )
        return (jnp.where(live_flag, moved, carried), None)

    return lax.scan(block_one_frame, identity_map, (blank_score, label_score, active))[0]


def log_apply(transfer, vector):
    return jax.nn.logsumexp(transfer + vector[None, :], axis=1)


def log_apply_back(transfer, vector):
    return jax.nn.logsumexp(transfer + vector[:, None], axis=0)


def log_combine(earlier, later):
    terms = later[..., :, :, None] + earlier[..., None, :, :]
    return jax.nn.logsumexp(terms, axis=-2)


def prefix_products(mats):
    count = mats.shape[-3]
    index = lax.broadcasted_iota(jnp.int32, (count, 1, 1), 0)
    step = 1
    while step < count:
        shifted = jnp.concatenate([mats[..., :step, :, :], mats[..., :-step, :, :]], axis=-3)
        mats = jnp.where(index >= step, log_combine(shifted, mats), mats)
        step *= 2
    return mats


def both_products(mats):
    backward = jnp.swapaxes(jnp.flip(mats, axis=0), -1, -2)
    scanned = prefix_products(jnp.stack([mats, backward]))
    return scanned[0], jnp.flip(scanned[1], axis=0)


def identity_of(places):
    row_ids = lax.broadcasted_iota(jnp.int32, (places, places), 0)
    col_ids = lax.broadcasted_iota(jnp.int32, (places, places), 1)
    return jnp.where(row_ids == col_ids, 0.0, NEG_BIG)


def frame_matrices(blank_score, label_score, active):
    frames, places = blank_score.shape
    partial = jnp.concatenate(
        [jnp.zeros((frames, 1), jnp.float32), jnp.cumsum(label_score, axis=1)], axis=1
    )
    row_ids = lax.broadcasted_iota(jnp.int32, (1, places, places), 1)
    col_ids = lax.broadcasted_iota(jnp.int32, (1, places, places), 2)
    moved = jnp.where(
        col_ids <= row_ids,
        blank_score[:, :, None] + partial[:, :, None] - partial[:, None, :],
        NEG_BIG,
    )
    return jnp.where(active[:, None, None], moved, identity_of(places)[None])


def ends_of(transfers, block_id, start_vec, finish_vec):
    places = start_vec.shape[0]
    forward, backward_t = both_products(transfers)
    eye = identity_of(places)[None]
    before = jnp.concatenate([eye, forward[:-1]], axis=0)[block_id]
    after_t = jnp.concatenate([backward_t[1:], eye], axis=0)[block_id]
    incoming = jax.nn.logsumexp(before + start_vec[None, :], axis=1)
    leaving = jax.nn.logsumexp(after_t + finish_vec[None, :], axis=1)
    return incoming, leaving


def frame_grads(mats, forward, backward_t, incoming, leaving, active):
    places = mats.shape[-1]
    reached = jax.nn.logsumexp(forward + incoming[None, None, :], axis=2)
    alpha = jnp.concatenate([incoming[None], reached[:-1]], axis=0)
    remaining = jax.nn.logsumexp(backward_t + leaving[None, None, :], axis=2)
    beta = jnp.concatenate([remaining[1:], leaving[None]], axis=0)
    joint = alpha[:, None, :] + mats + beta[:, :, None]
    frames = joint.shape[0]
    flat = jax.nn.softmax(joint.reshape(frames, places * places), axis=1)
    weights = jnp.where(active[:, None, None], flat.reshape(frames, places, places), 0.0)
    blank_grad = -jnp.sum(weights, axis=2)
    slot = lax.broadcasted_iota(jnp.int32, (places - 1, places, places), 0)
    row_ids = lax.broadcasted_iota(jnp.int32, (places - 1, places, places), 1)
    col_ids = lax.broadcasted_iota(jnp.int32, (places - 1, places, places), 2)
    cover = ((col_ids <= slot) & (slot < row_ids)).astype(jnp.float32)
    label_grad = -jnp.einsum("tkj,ikj->ti", weights, cover, precision=lax.Precision.HIGHEST)
    return blank_grad, label_grad


def joint_forward(frame_part, pred_here, label_row_ids, output_proj, output_bias):
    joined = jnp.tanh(frame_part.astype(jnp.float32)[:, None, :] + pred_here[None, :, :]).astype(
        jnp.bfloat16
    )
    frames_here, places, joint_width = joined.shape
    logits = (
        jnp.dot(
            joined.reshape(frames_here * places, joint_width),
            output_proj,
            preferred_element_type=jnp.float32,
        )
        + output_bias
    )
    logits = logits.reshape(frames_here, places, -1)
    exponent = jnp.exp(logits)
    denominator = jnp.sum(exponent, axis=-1, keepdims=True)
    log_total = jnp.log(denominator)[:, :, 0]
    blank_score = logits[:, :, 0] - log_total
    index_grid = jnp.broadcast_to(label_row_ids[None, :, None], (frames_here, places - 1, 1))
    picked = jnp.take_along_axis(logits[:, :-1, :], index_grid, axis=2)[:, :, 0]
    label_score = picked - log_total[:, :-1]
    posterior = exponent / denominator
    return (joined, posterior, blank_score, label_score)


def joint_backward(blank_grad, label_grad, label_row_ids, joined, posterior, output_proj):
    frames_here, places, vocab_size = posterior.shape
    label_full = jnp.pad(label_grad, ((0, 0), (0, 1)))
    weight_sum = blank_grad + label_full
    token_full = jnp.concatenate([label_row_ids, jnp.full((1,), -1, jnp.int32)])
    vocab_iota = lax.broadcasted_iota(jnp.int32, (1, 1, vocab_size), 2)
    blank_term = jnp.where(vocab_iota == 0, blank_grad[:, :, None], 0.0)
    label_term = jnp.where(vocab_iota == token_full[None, :, None], label_full[:, :, None], 0.0)
    logit_grad = -posterior * weight_sum[:, :, None] + blank_term + label_term
    logit_grad = logit_grad.astype(jnp.bfloat16).reshape(frames_here * places, vocab_size)
    joined_grad = lax.dot_general(
        logit_grad, output_proj, (((1,), (1,)), ((), ())), preferred_element_type=jnp.float32
    )
    joined_vals = joined.astype(jnp.float32).reshape(frames_here * places, -1)
    inner_grad = (joined_grad * (1.0 - joined_vals * joined_vals)).reshape(frames_here, places, -1)
    frame_part_grad = jnp.sum(inner_grad, axis=1).astype(jnp.bfloat16)
    pred_part_grad = jnp.sum(inner_grad, axis=0)
    return (frame_part_grad, pred_part_grad)


def network_sections(count):
    sections = []
    block_size = 2
    while block_size <= count:
        stride = block_size // 2
        while stride >= 1:
            sections.append((block_size, stride))
            stride = stride // 2
        block_size = block_size * 2
    return sections


def sort_section(keys, block_size, stride, device_id):
    count = keys.shape[0]
    position = jnp.arange(count, dtype=jnp.int32)
    partner = position ^ stride
    partner_keys = keys[partner]
    rising = position & block_size == 0
    lower_side = position < partner
    keep_small = lower_side == rising
    new_keys = jnp.where(
        keep_small, jnp.minimum(keys, partner_keys), jnp.maximum(keys, partner_keys)
    )
    takes = new_keys[device_id] != keys[device_id]
    return (new_keys, takes)


def route_owner(payload, keys, device_id, count):
    for block_size, stride in network_sections(count):
        keys, takes = sort_section(keys, block_size, stride, device_id)
        other = partner_2(payload, "joint", stride.bit_length() - 1)
        payload = jnp.where(takes, other, payload)
    return payload


def route_holder(payload, keys, device_id, count):
    for block_size, stride in network_sections(count):
        keys, takes = sort_section(keys, block_size, stride, device_id)
        other = partner_2(payload, "joint", stride.bit_length() - 1)
        payload = jnp.where(takes, other, payload)
    return payload


def route_rows(payload, source_of, axis):
    count = lax.axis_size(axis)
    rows = payload.shape[0]
    spread = lax.all_to_all(payload, axis, 0, 0, tiled=True)
    spread = spread.reshape(count, rows // count, *payload.shape[1:])
    picked = jnp.take(spread, source_of, axis=0).reshape(payload.shape)
    return lax.all_to_all(picked, axis, 0, 0, tiled=True)


def on_device(
    encoder_rows,
    up_weight,
    down_weight,
    encoder_proj,
    embedding,
    conv_taps,
    decoder_proj,
    output_proj,
    output_bias,
    frame_lengths,
    label_lengths,
    label_ids,
    owner_index,
):
    section_count = lax.axis_size("section")
    joint_count = lax.axis_size("joint")
    section_id = lax.axis_index("section")
    joint_id = lax.axis_index("joint")
    block_len = encoder_rows.shape[1]
    utterances = label_ids.shape[0]
    places = label_ids.shape[1] + 1
    own_rows = encoder_rows[0].astype(jnp.float32)
    normed_in = layer_norm(own_rows)[0].astype(jnp.bfloat16)
    gathered = lax.all_gather(normed_in, "section", axis=0, tiled=True)
    pre_hidden = jnp.dot(gathered, up_weight, preferred_element_type=jnp.float32)
    hidden = jax.nn.silu(pre_hidden).astype(jnp.bfloat16)
    encoded = own_rows + lax.psum_scatter(
        0.5 * jnp.dot(hidden, down_weight, preferred_element_type=jnp.float32),
        "section",
        scatter_dimension=0,
        tiled=True,
    )
    unit_rows, inv_scale = layer_norm(encoded)
    frame_part = jnp.dot(
        unit_rows.astype(jnp.bfloat16), encoder_proj, preferred_element_type=jnp.float32
    ).astype(jnp.bfloat16)
    order_iota = jnp.arange(utterances, dtype=jnp.int32)
    inverse = jnp.zeros((utterances,), jnp.int32).at[owner_index].set(order_iota)
    own_utterance = inverse[joint_id]
    owner_frames = route_rows(frame_part, inverse, "joint")
    context = jnp.concatenate([jnp.zeros((utterances, 1), jnp.int32), label_ids], axis=1)
    vocab_rows = embedding.shape[0]
    vocab_ids = joint_id * vocab_rows + jnp.arange(vocab_rows, dtype=jnp.int32)

    def label_term(start_row, row_count):
        number = row_count // places
        wanted = context[inverse].reshape(number * places)
        selector = (wanted[:, None] == vocab_ids[None, :]).astype(jnp.bfloat16)
        return jnp.dot(selector, embedding, preferred_element_type=jnp.float32)

    looked = lax.psum_scatter(
        label_term(jnp.int32(0), places * lax.axis_size("joint")).astype(jnp.bfloat16),
        "joint",
        scatter_dimension=0,
        tiled=True,
    ).astype(jnp.float32)
    previous = jnp.concatenate([looked[:1], looked[:-1]], axis=0)
    pred_act = jnp.maximum(conv_taps[0] * previous + conv_taps[1] * looked, 0.0).astype(
        jnp.bfloat16
    )
    pred_rows = jnp.dot(pred_act, decoder_proj, preferred_element_type=jnp.float32)
    label_here = label_ids[own_utterance]
    frames_used = frame_lengths[own_utterance]
    labels_used = label_lengths[own_utterance]
    joined, posterior, blank_score, label_score = joint_forward(
        owner_frames, pred_rows, label_here, output_proj, output_bias
    )
    frame_ids = section_id * block_len + jnp.arange(block_len, dtype=jnp.int32)
    active = frame_ids < frames_used
    mats = frame_matrices(blank_score, label_score, active)
    forward, backward_t = both_products(mats)
    transfers = lax.all_to_all(
        jnp.broadcast_to(forward[-1][None], (section_count,) + forward.shape[1:]),
        "section",
        0,
        0,
        tiled=True,
    )
    place_iota = jnp.arange(places, dtype=jnp.int32)
    start_vec = jnp.where(place_iota == 0, 0.0, NEG_BIG)
    finish_vec = jnp.where(place_iota == labels_used, 0.0, NEG_BIG)
    incoming, leaving = ends_of(transfers, section_id, start_vec, finish_vec)
    blank_grad, label_grad = frame_grads(mats, forward, backward_t, incoming, leaving, active)
    frame_part_grad, pred_part = joint_backward(
        blank_grad, label_grad, label_here, joined, posterior, output_proj
    )
    part_grad = route_rows(frame_part_grad, owner_index, "joint")
    unit_grad = lax.dot_general(
        part_grad, encoder_proj, (((1,), (1,)), ((), ())), preferred_element_type=jnp.float32
    )
    first_mean = jnp.mean(unit_grad, axis=-1, keepdims=True)
    second_mean = jnp.mean(unit_grad * unit_rows, axis=-1, keepdims=True)
    row_grad = (inv_scale * (unit_grad - first_mean - unit_rows * second_mean)).astype(jnp.bfloat16)
    grad_all = lax.all_gather(row_grad, "section", axis=0, tiled=True)
    hidden_grad = 0.5 * lax.dot_general(
        grad_all, down_weight, (((1,), (1,)), ((), ())), preferred_element_type=jnp.float32
    )
    gate_sigmoid = jax.nn.sigmoid(pre_hidden)
    pre_grad = (hidden_grad * gate_sigmoid * (1.0 + pre_hidden * (1.0 - gate_sigmoid))).astype(
        jnp.bfloat16
    )
    up_part = lax.dot_general(
        gathered, pre_grad, (((0,), (0,)), ((), ())), preferred_element_type=jnp.float32
    )
    down_part = 0.5 * lax.dot_general(
        hidden, grad_all, (((0,), (0,)), ((), ())), preferred_element_type=jnp.float32
    )
    weight_parts = jnp.concatenate([up_part, down_part.T], axis=1).astype(jnp.bfloat16)
    weight_pieces = lax.all_to_all(weight_parts, "joint", 0, 0, tiled=True)
    weight_sums = jnp.sum(
        weight_pieces.reshape(joint_count, -1, weight_parts.shape[1]).astype(jnp.float32), axis=0
    )
    hidden_here = up_part.shape[1]
    up_sum = weight_sums[:, :hidden_here]
    down_sum = weight_sums[:, hidden_here:].T
    pred_pieces = jnp.swapaxes(pred_part.reshape(places, section_count, -1), 0, 1)
    pred_sum = jnp.sum(lax.all_to_all(pred_pieces, "section", 0, 0, tiled=True), axis=0)[None]
    return (row_grad[None], up_sum, down_sum, pred_sum)


def solution(mesh):
    return jax.shard_map(
        on_device,
        mesh=mesh,
        in_specs=(
            P("joint", "section", None),
            P(None, "section"),
            P("section", None),
            P(),
            P("joint", None),
            P(),
            P(),
            P(),
            P(),
            P(),
            P(),
            P(),
            P(),
        ),
        out_specs=(
            P("joint", "section", None),
            P("joint", "section"),
            P("section", "joint"),
            P("joint", None, "section"),
        ),
        check_vma=False,
    )
```

```python
import jax
import jax.numpy as jnp
from jax import lax
from jax.sharding import PartitionSpec as P

NEG_BIG = -1000000000.0


def partner_2(block, axis, bit):
    count = lax.axis_size(axis)
    route = []
    for low in range(count):
        high = low | 1 << bit
        if high != low and high < count:
            route += [(low, high), (high, low)]
    return lax.ppermute(block, axis, route)


def from_behind(value, axis, steps):
    count = lax.axis_size(axis)
    initial, last = (max(0, -steps), min(count, count - steps))
    return lax.ppermute(value, axis, [(source, source + steps) for source in range(initial, last)])


def layer_norm(values):
    average = jnp.mean(values, axis=-1, keepdims=True)
    centered = values - average
    variance = jnp.mean(centered * centered, axis=-1, keepdims=True)
    inv_scale = lax.rsqrt(variance + 1e-05)
    return (centered * inv_scale, inv_scale)


def lower_paths(label_row):
    partial_sums = jnp.concatenate([jnp.zeros((1,), jnp.float32), jnp.cumsum(label_row)])
    places = partial_sums.shape[0]
    row_ids = lax.broadcasted_iota(jnp.int32, (places, places), 0)
    col_ids = lax.broadcasted_iota(jnp.int32, (places, places), 1)
    return jnp.where(col_ids <= row_ids, partial_sums[:, None] - partial_sums[None, :], NEG_BIG)


def advance(vector, blank_row, label_row, active):
    moved = blank_row + jax.nn.logsumexp(lower_paths(label_row) + vector[None, :], axis=1)
    return jnp.where(active, moved, vector)


def run_block(vector, blank_score, label_score, active):

    def run_one_frame(carried, inputs):
        blank_row, label_row, live_flag = inputs
        return (advance(carried, blank_row, label_row, live_flag), None)

    return lax.scan(run_one_frame, vector, (blank_score, label_score, active))[0]


def block_matrix(blank_score, label_score, active):
    places = blank_score.shape[1]
    row_ids = lax.broadcasted_iota(jnp.int32, (places, places), 0)
    col_ids = lax.broadcasted_iota(jnp.int32, (places, places), 1)
    identity_map = jnp.where(row_ids == col_ids, 0.0, NEG_BIG)

    def block_one_frame(carried, inputs):
        blank_row, label_row, live_flag = inputs
        moved = blank_row[:, None] + jax.nn.logsumexp(
            lower_paths(label_row)[:, :, None] + carried[None, :, :], axis=1
        )
        return (jnp.where(live_flag, moved, carried), None)

    return lax.scan(block_one_frame, identity_map, (blank_score, label_score, active))[0]


def log_apply(transfer, vector):
    return jax.nn.logsumexp(transfer + vector[None, :], axis=1)


def log_apply_back(transfer, vector):
    return jax.nn.logsumexp(transfer + vector[:, None], axis=0)


def log_combine(earlier, later):
    terms = later[..., :, :, None] + earlier[..., None, :, :]
    return jax.nn.logsumexp(terms, axis=-2)


def prefix_products(mats):
    count = mats.shape[-3]
    index = lax.broadcasted_iota(jnp.int32, (count, 1, 1), 0)
    step = 1
    while step < count:
        shifted = jnp.concatenate([mats[..., :step, :, :], mats[..., :-step, :, :]], axis=-3)
        mats = jnp.where(index >= step, log_combine(shifted, mats), mats)
        step *= 2
    return mats


def both_products(mats):
    backward = jnp.swapaxes(jnp.flip(mats, axis=0), -1, -2)
    scanned = prefix_products(jnp.stack([mats, backward]))
    return scanned[0], jnp.flip(scanned[1], axis=0)


def identity_of(places):
    row_ids = lax.broadcasted_iota(jnp.int32, (places, places), 0)
    col_ids = lax.broadcasted_iota(jnp.int32, (places, places), 1)
    return jnp.where(row_ids == col_ids, 0.0, NEG_BIG)


def frame_matrices(blank_score, label_score, active):
    frames, places = blank_score.shape
    partial = jnp.concatenate(
        [jnp.zeros((frames, 1), jnp.float32), jnp.cumsum(label_score, axis=1)], axis=1
    )
    row_ids = lax.broadcasted_iota(jnp.int32, (1, places, places), 1)
    col_ids = lax.broadcasted_iota(jnp.int32, (1, places, places), 2)
    moved = jnp.where(
        col_ids <= row_ids,
        blank_score[:, :, None] + partial[:, :, None] - partial[:, None, :],
        NEG_BIG,
    )
    return jnp.where(active[:, None, None], moved, identity_of(places)[None])


def ends_of(transfers, block_id, start_vec, finish_vec):
    places = start_vec.shape[0]
    forward, backward_t = both_products(transfers)
    eye = identity_of(places)[None]
    before = jnp.concatenate([eye, forward[:-1]], axis=0)[block_id]
    after_t = jnp.concatenate([backward_t[1:], eye], axis=0)[block_id]
    incoming = jax.nn.logsumexp(before + start_vec[None, :], axis=1)
    leaving = jax.nn.logsumexp(after_t + finish_vec[None, :], axis=1)
    return incoming, leaving


def frame_grads(mats, forward, backward_t, incoming, leaving, active):
    places = mats.shape[-1]
    reached = jax.nn.logsumexp(forward + incoming[None, None, :], axis=2)
    alpha = jnp.concatenate([incoming[None], reached[:-1]], axis=0)
    remaining = jax.nn.logsumexp(backward_t + leaving[None, None, :], axis=2)
    beta = jnp.concatenate([remaining[1:], leaving[None]], axis=0)
    joint = alpha[:, None, :] + mats + beta[:, :, None]
    frames = joint.shape[0]
    flat = jax.nn.softmax(joint.reshape(frames, places * places), axis=1)
    weights = jnp.where(active[:, None, None], flat.reshape(frames, places, places), 0.0)
    blank_grad = -jnp.sum(weights, axis=2)
    slot = lax.broadcasted_iota(jnp.int32, (places - 1, places, places), 0)
    row_ids = lax.broadcasted_iota(jnp.int32, (places - 1, places, places), 1)
    col_ids = lax.broadcasted_iota(jnp.int32, (places - 1, places, places), 2)
    cover = ((col_ids <= slot) & (slot < row_ids)).astype(jnp.float32)
    label_grad = -jnp.einsum("tkj,ikj->ti", weights, cover, precision=lax.Precision.HIGHEST)
    return blank_grad, label_grad


def joint_forward(frame_part, pred_here, label_row_ids, output_proj, output_bias):
    joined = jnp.tanh(frame_part.astype(jnp.float32)[:, None, :] + pred_here[None, :, :]).astype(
        jnp.bfloat16
    )
    frames_here, places, joint_width = joined.shape
    logits = (
        jnp.dot(
            joined.reshape(frames_here * places, joint_width),
            output_proj,
            preferred_element_type=jnp.float32,
        )
        + output_bias
    )
    logits = logits.reshape(frames_here, places, -1)
    exponent = jnp.exp(logits)
    denominator = jnp.sum(exponent, axis=-1, keepdims=True)
    log_total = jnp.log(denominator)[:, :, 0]
    blank_score = logits[:, :, 0] - log_total
    index_grid = jnp.broadcast_to(label_row_ids[None, :, None], (frames_here, places - 1, 1))
    picked = jnp.take_along_axis(logits[:, :-1, :], index_grid, axis=2)[:, :, 0]
    label_score = picked - log_total[:, :-1]
    posterior = exponent / denominator
    return (joined, posterior, blank_score, label_score)


def joint_backward(blank_grad, label_grad, label_row_ids, joined, posterior, output_proj):
    frames_here, places, vocab_size = posterior.shape
    label_full = jnp.pad(label_grad, ((0, 0), (0, 1)))
    weight_sum = blank_grad + label_full
    token_full = jnp.concatenate([label_row_ids, jnp.full((1,), -1, jnp.int32)])
    vocab_iota = lax.broadcasted_iota(jnp.int32, (1, 1, vocab_size), 2)
    blank_term = jnp.where(vocab_iota == 0, blank_grad[:, :, None], 0.0)
    label_term = jnp.where(vocab_iota == token_full[None, :, None], label_full[:, :, None], 0.0)
    logit_grad = -posterior * weight_sum[:, :, None] + blank_term + label_term
    logit_grad = logit_grad.astype(jnp.bfloat16).reshape(frames_here * places, vocab_size)
    joined_grad = lax.dot_general(
        logit_grad, output_proj, (((1,), (1,)), ((), ())), preferred_element_type=jnp.float32
    )
    joined_vals = joined.astype(jnp.float32).reshape(frames_here * places, -1)
    inner_grad = (joined_grad * (1.0 - joined_vals * joined_vals)).reshape(frames_here, places, -1)
    frame_part_grad = jnp.sum(inner_grad, axis=1).astype(jnp.bfloat16)
    pred_part_grad = jnp.sum(inner_grad, axis=0)
    return (frame_part_grad, pred_part_grad)


def network_sections(count):
    sections = []
    block_size = 2
    while block_size <= count:
        stride = block_size // 2
        while stride >= 1:
            sections.append((block_size, stride))
            stride = stride // 2
        block_size = block_size * 2
    return sections


def sort_section(keys, block_size, stride, device_id):
    count = keys.shape[0]
    position = jnp.arange(count, dtype=jnp.int32)
    partner = position ^ stride
    partner_keys = keys[partner]
    rising = position & block_size == 0
    lower_side = position < partner
    keep_small = lower_side == rising
    new_keys = jnp.where(
        keep_small, jnp.minimum(keys, partner_keys), jnp.maximum(keys, partner_keys)
    )
    takes = new_keys[device_id] != keys[device_id]
    return (new_keys, takes)


def route_owner(payload, keys, device_id, count):
    for block_size, stride in network_sections(count):
        keys, takes = sort_section(keys, block_size, stride, device_id)
        other = partner_2(payload, "joint", stride.bit_length() - 1)
        payload = jnp.where(takes, other, payload)
    return payload


def route_holder(payload, keys, device_id, count):
    for block_size, stride in network_sections(count):
        keys, takes = sort_section(keys, block_size, stride, device_id)
        other = partner_2(payload, "joint", stride.bit_length() - 1)
        payload = jnp.where(takes, other, payload)
    return payload


def route_rows(payload, source_of, axis):
    count = lax.axis_size(axis)
    rows = payload.shape[0]
    spread = lax.all_to_all(payload, axis, 0, 0, tiled=True)
    spread = spread.reshape(count, rows // count, *payload.shape[1:])
    picked = jnp.take(spread, source_of, axis=0).reshape(payload.shape)
    return lax.all_to_all(picked, axis, 0, 0, tiled=True)


def on_device(
    encoder_rows,
    up_weight,
    down_weight,
    encoder_proj,
    embedding,
    conv_taps,
    decoder_proj,
    output_proj,
    output_bias,
    frame_lengths,
    label_lengths,
    label_ids,
    owner_index,
):
    section_count = lax.axis_size("section")
    joint_count = lax.axis_size("joint")
    section_id = lax.axis_index("section")
    joint_id = lax.axis_index("joint")
    block_len = encoder_rows.shape[1]
    utterances = label_ids.shape[0]
    places = label_ids.shape[1] + 1
    own_rows = encoder_rows[0].astype(jnp.float32)
    normed_in = layer_norm(own_rows)[0].astype(jnp.bfloat16)
    gathered = lax.all_gather(normed_in, "section", axis=0, tiled=True)
    pre_hidden = jnp.dot(gathered, up_weight, preferred_element_type=jnp.float32)
    hidden = jax.nn.silu(pre_hidden).astype(jnp.bfloat16)
    output_pieces = lax.all_to_all(
        0.5 * jnp.dot(hidden, down_weight, preferred_element_type=jnp.float32),
        "section",
        0,
        0,
        tiled=True,
    )
    encoded = own_rows + jnp.sum(output_pieces.reshape(section_count, block_len, -1), axis=0)
    unit_rows, inv_scale = layer_norm(encoded)
    frame_part = jnp.dot(
        unit_rows.astype(jnp.bfloat16), encoder_proj, preferred_element_type=jnp.float32
    ).astype(jnp.bfloat16)
    order_iota = jnp.arange(utterances, dtype=jnp.int32)
    inverse = jnp.zeros((utterances,), jnp.int32).at[owner_index].set(order_iota)
    own_utterance = inverse[joint_id]
    owner_frames = route_rows(frame_part, inverse, "joint")
    context = jnp.concatenate([jnp.zeros((utterances, 1), jnp.int32), label_ids], axis=1)
    vocab_rows = embedding.shape[0]
    vocab_ids = joint_id * vocab_rows + jnp.arange(vocab_rows, dtype=jnp.int32)

    def label_term(start_row, row_count):
        number = row_count // places
        wanted = context[inverse].reshape(number * places)
        selector = (wanted[:, None] == vocab_ids[None, :]).astype(jnp.bfloat16)
        return jnp.dot(selector, embedding, preferred_element_type=jnp.float32)

    looked_pieces = lax.all_to_all(
        label_term(jnp.int32(0), places * joint_count).astype(jnp.bfloat16), "joint", 0, 0, tiled=True
    )
    looked = jnp.sum(looked_pieces.reshape(joint_count, places, -1).astype(jnp.float32), axis=0)
    previous = jnp.concatenate([looked[:1], looked[:-1]], axis=0)
    pred_act = jnp.maximum(conv_taps[0] * previous + conv_taps[1] * looked, 0.0).astype(
        jnp.bfloat16
    )
    pred_rows = jnp.dot(pred_act, decoder_proj, preferred_element_type=jnp.float32)
    label_here = label_ids[own_utterance]
    frames_used = frame_lengths[own_utterance]
    labels_used = label_lengths[own_utterance]
    joined, posterior, blank_score, label_score = joint_forward(
        owner_frames, pred_rows, label_here, output_proj, output_bias
    )
    frame_ids = section_id * block_len + jnp.arange(block_len, dtype=jnp.int32)
    active = frame_ids < frames_used
    mats = frame_matrices(blank_score, label_score, active)
    forward, backward_t = both_products(mats)
    transfers = lax.all_to_all(
        jnp.broadcast_to(forward[-1][None], (section_count,) + forward.shape[1:]),
        "section",
        0,
        0,
        tiled=True,
    )
    place_iota = jnp.arange(places, dtype=jnp.int32)
    start_vec = jnp.where(place_iota == 0, 0.0, NEG_BIG)
    finish_vec = jnp.where(place_iota == labels_used, 0.0, NEG_BIG)
    incoming, leaving = ends_of(transfers, section_id, start_vec, finish_vec)
    blank_grad, label_grad = frame_grads(mats, forward, backward_t, incoming, leaving, active)
    frame_part_grad, pred_part = joint_backward(
        blank_grad, label_grad, label_here, joined, posterior, output_proj
    )
    part_grad = route_rows(frame_part_grad, owner_index, "joint")
    unit_grad = lax.dot_general(
        part_grad, encoder_proj, (((1,), (1,)), ((), ())), preferred_element_type=jnp.float32
    )
    first_mean = jnp.mean(unit_grad, axis=-1, keepdims=True)
    second_mean = jnp.mean(unit_grad * unit_rows, axis=-1, keepdims=True)
    row_grad = (inv_scale * (unit_grad - first_mean - unit_rows * second_mean)).astype(jnp.bfloat16)
    grad_all = lax.all_gather(row_grad, "section", axis=0, tiled=True)
    hidden_grad = 0.5 * lax.dot_general(
        grad_all, down_weight, (((1,), (1,)), ((), ())), preferred_element_type=jnp.float32
    )
    gate_sigmoid = jax.nn.sigmoid(pre_hidden)
    pre_grad = (hidden_grad * gate_sigmoid * (1.0 + pre_hidden * (1.0 - gate_sigmoid))).astype(
        jnp.bfloat16
    )
    up_part = lax.dot_general(
        gathered, pre_grad, (((0,), (0,)), ((), ())), preferred_element_type=jnp.float32
    )
    down_part = 0.5 * lax.dot_general(
        hidden, grad_all, (((0,), (0,)), ((), ())), preferred_element_type=jnp.float32
    )
    weight_parts = jnp.concatenate([up_part, down_part.T], axis=1).astype(jnp.bfloat16)
    weight_pieces = lax.all_to_all(weight_parts, "joint", 0, 0, tiled=True)
    weight_sums = jnp.sum(
        weight_pieces.reshape(joint_count, -1, weight_parts.shape[1]).astype(jnp.float32), axis=0
    )
    hidden_here = up_part.shape[1]
    up_sum = weight_sums[:, :hidden_here]
    down_sum = weight_sums[:, hidden_here:].T
    pred_pieces = jnp.swapaxes(pred_part.reshape(places, section_count, -1), 0, 1)
    pred_sum = jnp.sum(lax.all_to_all(pred_pieces, "section", 0, 0, tiled=True), axis=0)[None]
    return (row_grad[None], up_sum, down_sum, pred_sum)


def solution(mesh):
    return jax.shard_map(
        on_device,
        mesh=mesh,
        in_specs=(
            P("joint", "section", None),
            P(None, "section"),
            P("section", None),
            P(),
            P("joint", None),
            P(),
            P(),
            P(),
            P(),
            P(),
            P(),
            P(),
            P(),
        ),
        out_specs=(
            P("joint", "section", None),
            P("joint", "section"),
            P("section", "joint"),
            P("joint", None, "section"),
        ),
        check_vma=False,
    )
```

```python
import jax
import jax.numpy as jnp
from jax import lax
from jax.sharding import PartitionSpec as P

NEG_BIG = -1000000000.0


def partner_2(block, axis, bit):
    count = lax.axis_size(axis)
    route = []
    for low in range(count):
        high = low | 1 << bit
        if high != low and high < count:
            route += [(low, high), (high, low)]
    return lax.ppermute(block, axis, route)


def from_behind(value, axis, steps):
    count = lax.axis_size(axis)
    initial, last = (max(0, -steps), min(count, count - steps))
    return lax.ppermute(value, axis, [(source, source + steps) for source in range(initial, last)])


def layer_norm(values):
    average = jnp.mean(values, axis=-1, keepdims=True)
    centered = values - average
    variance = jnp.mean(centered * centered, axis=-1, keepdims=True)
    inv_scale = lax.rsqrt(variance + 1e-05)
    return (centered * inv_scale, inv_scale)


def lower_paths(label_row):
    partial_sums = jnp.concatenate([jnp.zeros((1,), jnp.float32), jnp.cumsum(label_row)])
    places = partial_sums.shape[0]
    row_ids = lax.broadcasted_iota(jnp.int32, (places, places), 0)
    col_ids = lax.broadcasted_iota(jnp.int32, (places, places), 1)
    return jnp.where(col_ids <= row_ids, partial_sums[:, None] - partial_sums[None, :], NEG_BIG)


def advance(vector, blank_row, label_row, active):
    moved = blank_row + jax.nn.logsumexp(lower_paths(label_row) + vector[None, :], axis=1)
    return jnp.where(active, moved, vector)


def run_block(vector, blank_score, label_score, active):

    def run_one_frame(carried, inputs):
        blank_row, label_row, live_flag = inputs
        return (advance(carried, blank_row, label_row, live_flag), None)

    return lax.scan(run_one_frame, vector, (blank_score, label_score, active))[0]


def block_matrix(blank_score, label_score, active):
    places = blank_score.shape[1]
    row_ids = lax.broadcasted_iota(jnp.int32, (places, places), 0)
    col_ids = lax.broadcasted_iota(jnp.int32, (places, places), 1)
    identity_map = jnp.where(row_ids == col_ids, 0.0, NEG_BIG)

    def block_one_frame(carried, inputs):
        blank_row, label_row, live_flag = inputs
        moved = blank_row[:, None] + jax.nn.logsumexp(
            lower_paths(label_row)[:, :, None] + carried[None, :, :], axis=1
        )
        return (jnp.where(live_flag, moved, carried), None)

    return lax.scan(block_one_frame, identity_map, (blank_score, label_score, active))[0]


def log_apply(transfer, vector):
    return jax.nn.logsumexp(transfer + vector[None, :], axis=1)


def log_apply_back(transfer, vector):
    return jax.nn.logsumexp(transfer + vector[:, None], axis=0)


def log_combine(earlier, later):
    terms = later[..., :, :, None] + earlier[..., None, :, :]
    return jax.nn.logsumexp(terms, axis=-2)


def prefix_products(mats):
    count = mats.shape[-3]
    index = lax.broadcasted_iota(jnp.int32, (count, 1, 1), 0)
    step = 1
    while step < count:
        shifted = jnp.concatenate([mats[..., :step, :, :], mats[..., :-step, :, :]], axis=-3)
        mats = jnp.where(index >= step, log_combine(shifted, mats), mats)
        step *= 2
    return mats


def both_products(mats):
    backward = jnp.swapaxes(jnp.flip(mats, axis=0), -1, -2)
    scanned = prefix_products(jnp.stack([mats, backward]))
    return scanned[0], jnp.flip(scanned[1], axis=0)


def identity_of(places):
    row_ids = lax.broadcasted_iota(jnp.int32, (places, places), 0)
    col_ids = lax.broadcasted_iota(jnp.int32, (places, places), 1)
    return jnp.where(row_ids == col_ids, 0.0, NEG_BIG)


def frame_matrices(blank_score, label_score, active):
    frames, places = blank_score.shape
    partial = jnp.concatenate(
        [jnp.zeros((frames, 1), jnp.float32), jnp.cumsum(label_score, axis=1)], axis=1
    )
    row_ids = lax.broadcasted_iota(jnp.int32, (1, places, places), 1)
    col_ids = lax.broadcasted_iota(jnp.int32, (1, places, places), 2)
    moved = jnp.where(
        col_ids <= row_ids,
        blank_score[:, :, None] + partial[:, :, None] - partial[:, None, :],
        NEG_BIG,
    )
    return jnp.where(active[:, None, None], moved, identity_of(places)[None])


def ends_of(transfers, block_id, start_vec, finish_vec):
    places = start_vec.shape[0]
    forward, backward_t = both_products(transfers)
    eye = identity_of(places)[None]
    before = jnp.concatenate([eye, forward[:-1]], axis=0)[block_id]
    after_t = jnp.concatenate([backward_t[1:], eye], axis=0)[block_id]
    incoming = jax.nn.logsumexp(before + start_vec[None, :], axis=1)
    leaving = jax.nn.logsumexp(after_t + finish_vec[None, :], axis=1)
    return incoming, leaving


def frame_grads(mats, forward, backward_t, incoming, leaving, active):
    places = mats.shape[-1]
    reached = jax.nn.logsumexp(forward + incoming[None, None, :], axis=2)
    alpha = jnp.concatenate([incoming[None], reached[:-1]], axis=0)
    remaining = jax.nn.logsumexp(backward_t + leaving[None, None, :], axis=2)
    beta = jnp.concatenate([remaining[1:], leaving[None]], axis=0)
    joint = alpha[:, None, :] + mats + beta[:, :, None]
    frames = joint.shape[0]
    flat = jax.nn.softmax(joint.reshape(frames, places * places), axis=1)
    weights = jnp.where(active[:, None, None], flat.reshape(frames, places, places), 0.0)
    blank_grad = -jnp.sum(weights, axis=2)
    slot = lax.broadcasted_iota(jnp.int32, (places - 1, places, places), 0)
    row_ids = lax.broadcasted_iota(jnp.int32, (places - 1, places, places), 1)
    col_ids = lax.broadcasted_iota(jnp.int32, (places - 1, places, places), 2)
    cover = ((col_ids <= slot) & (slot < row_ids)).astype(jnp.float32)
    label_grad = -jnp.einsum("tkj,ikj->ti", weights, cover, precision=lax.Precision.HIGHEST)
    return blank_grad, label_grad


def joint_forward(frame_part, pred_here, label_row_ids, output_proj, output_bias):
    joined = jnp.tanh(frame_part.astype(jnp.float32)[:, None, :] + pred_here[None, :, :]).astype(
        jnp.bfloat16
    )
    frames_here, places, joint_width = joined.shape
    logits = (
        jnp.dot(
            joined.reshape(frames_here * places, joint_width),
            output_proj,
            preferred_element_type=jnp.float32,
        )
        + output_bias
    )
    logits = logits.reshape(frames_here, places, -1)
    exponent = jnp.exp(logits)
    denominator = jnp.sum(exponent, axis=-1, keepdims=True)
    log_total = jnp.log(denominator)[:, :, 0]
    blank_score = logits[:, :, 0] - log_total
    index_grid = jnp.broadcast_to(label_row_ids[None, :, None], (frames_here, places - 1, 1))
    picked = jnp.take_along_axis(logits[:, :-1, :], index_grid, axis=2)[:, :, 0]
    label_score = picked - log_total[:, :-1]
    posterior = exponent / denominator
    return (joined, posterior, blank_score, label_score)


def joint_backward(blank_grad, label_grad, label_row_ids, joined, posterior, output_proj):
    frames_here, places, vocab_size = posterior.shape
    label_full = jnp.pad(label_grad, ((0, 0), (0, 1)))
    weight_sum = blank_grad + label_full
    token_full = jnp.concatenate([label_row_ids, jnp.full((1,), -1, jnp.int32)])
    vocab_iota = lax.broadcasted_iota(jnp.int32, (1, 1, vocab_size), 2)
    blank_term = jnp.where(vocab_iota == 0, blank_grad[:, :, None], 0.0)
    label_term = jnp.where(vocab_iota == token_full[None, :, None], label_full[:, :, None], 0.0)
    logit_grad = -posterior * weight_sum[:, :, None] + blank_term + label_term
    logit_grad = logit_grad.astype(jnp.bfloat16).reshape(frames_here * places, vocab_size)
    joined_grad = lax.dot_general(
        logit_grad, output_proj, (((1,), (1,)), ((), ())), preferred_element_type=jnp.float32
    )
    joined_vals = joined.astype(jnp.float32).reshape(frames_here * places, -1)
    inner_grad = (joined_grad * (1.0 - joined_vals * joined_vals)).reshape(frames_here, places, -1)
    frame_part_grad = jnp.sum(inner_grad, axis=1).astype(jnp.bfloat16)
    pred_part_grad = jnp.sum(inner_grad, axis=0)
    return (frame_part_grad, pred_part_grad)


def network_sections(count):
    sections = []
    block_size = 2
    while block_size <= count:
        stride = block_size // 2
        while stride >= 1:
            sections.append((block_size, stride))
            stride = stride // 2
        block_size = block_size * 2
    return sections


def sort_section(keys, block_size, stride, device_id):
    count = keys.shape[0]
    position = jnp.arange(count, dtype=jnp.int32)
    partner = position ^ stride
    partner_keys = keys[partner]
    rising = position & block_size == 0
    lower_side = position < partner
    keep_small = lower_side == rising
    new_keys = jnp.where(
        keep_small, jnp.minimum(keys, partner_keys), jnp.maximum(keys, partner_keys)
    )
    takes = new_keys[device_id] != keys[device_id]
    return (new_keys, takes)


def route_owner(payload, keys, device_id, count):
    for block_size, stride in network_sections(count):
        keys, takes = sort_section(keys, block_size, stride, device_id)
        other = partner_2(payload, "joint", stride.bit_length() - 1)
        payload = jnp.where(takes, other, payload)
    return payload


def route_holder(payload, keys, device_id, count):
    for block_size, stride in network_sections(count):
        keys, takes = sort_section(keys, block_size, stride, device_id)
        other = partner_2(payload, "joint", stride.bit_length() - 1)
        payload = jnp.where(takes, other, payload)
    return payload


def route_rows(payload, source_of, axis):
    count = lax.axis_size(axis)
    rows = payload.shape[0]
    spread = lax.all_to_all(payload, axis, 0, 0, tiled=True)
    spread = spread.reshape(count, rows // count, *payload.shape[1:])
    picked = jnp.take(spread, source_of, axis=0).reshape(payload.shape)
    return lax.all_to_all(picked, axis, 0, 0, tiled=True)


def on_device(
    encoder_rows,
    up_weight,
    down_weight,
    encoder_proj,
    embedding,
    conv_taps,
    decoder_proj,
    output_proj,
    output_bias,
    frame_lengths,
    label_lengths,
    label_ids,
    owner_index,
):
    section_count = lax.axis_size("section")
    joint_count = lax.axis_size("joint")
    section_id = lax.axis_index("section")
    joint_id = lax.axis_index("joint")
    block_len = encoder_rows.shape[1]
    utterances = label_ids.shape[0]
    places = label_ids.shape[1] + 1
    own_rows = encoder_rows[0].astype(jnp.float32)
    normed_in = layer_norm(own_rows)[0].astype(jnp.bfloat16)
    gathered = lax.all_gather(normed_in, "section", axis=0, tiled=True)
    pre_hidden = jnp.dot(gathered, up_weight, preferred_element_type=jnp.float32)
    hidden = jax.nn.silu(pre_hidden).astype(jnp.bfloat16)
    encoded = own_rows + lax.psum_scatter(
        0.5 * jnp.dot(hidden, down_weight, preferred_element_type=jnp.float32),
        "section",
        scatter_dimension=0,
        tiled=True,
    )
    unit_rows, inv_scale = layer_norm(encoded)
    frame_part = jnp.dot(
        unit_rows.astype(jnp.bfloat16), encoder_proj, preferred_element_type=jnp.float32
    ).astype(jnp.bfloat16)
    order_iota = jnp.arange(utterances, dtype=jnp.int32)
    inverse = jnp.zeros((utterances,), jnp.int32).at[owner_index].set(order_iota)
    own_utterance = inverse[joint_id]
    owner_frames = route_rows(frame_part, inverse, "joint")
    context = jnp.concatenate([jnp.zeros((utterances, 1), jnp.int32), label_ids], axis=1)
    vocab_rows = embedding.shape[0]
    vocab_ids = joint_id * vocab_rows + jnp.arange(vocab_rows, dtype=jnp.int32)

    def label_term(start_row, row_count):
        number = row_count // places
        wanted = context[inverse].reshape(number * places)
        selector = (wanted[:, None] == vocab_ids[None, :]).astype(jnp.bfloat16)
        return jnp.dot(selector, embedding, preferred_element_type=jnp.float32)

    looked_pieces = lax.all_to_all(
        label_term(jnp.int32(0), places * joint_count).astype(jnp.bfloat16), "joint", 0, 0, tiled=True
    )
    looked = jnp.sum(looked_pieces.reshape(joint_count, places, -1).astype(jnp.float32), axis=0)
    previous = jnp.concatenate([looked[:1], looked[:-1]], axis=0)
    pred_act = jnp.maximum(conv_taps[0] * previous + conv_taps[1] * looked, 0.0).astype(
        jnp.bfloat16
    )
    pred_rows = jnp.dot(pred_act, decoder_proj, preferred_element_type=jnp.float32)
    label_here = label_ids[own_utterance]
    frames_used = frame_lengths[own_utterance]
    labels_used = label_lengths[own_utterance]
    joined, posterior, blank_score, label_score = joint_forward(
        owner_frames, pred_rows, label_here, output_proj, output_bias
    )
    frame_ids = section_id * block_len + jnp.arange(block_len, dtype=jnp.int32)
    active = frame_ids < frames_used
    mats = frame_matrices(blank_score, label_score, active)
    forward, backward_t = both_products(mats)
    transfers = lax.all_to_all(
        jnp.broadcast_to(forward[-1][None], (section_count,) + forward.shape[1:]),
        "section",
        0,
        0,
        tiled=True,
    )
    place_iota = jnp.arange(places, dtype=jnp.int32)
    start_vec = jnp.where(place_iota == 0, 0.0, NEG_BIG)
    finish_vec = jnp.where(place_iota == labels_used, 0.0, NEG_BIG)
    incoming, leaving = ends_of(transfers, section_id, start_vec, finish_vec)
    blank_grad, label_grad = frame_grads(mats, forward, backward_t, incoming, leaving, active)
    frame_part_grad, pred_part = joint_backward(
        blank_grad, label_grad, label_here, joined, posterior, output_proj
    )
    part_grad = route_rows(frame_part_grad, owner_index, "joint")
    unit_grad = lax.dot_general(
        part_grad, encoder_proj, (((1,), (1,)), ((), ())), preferred_element_type=jnp.float32
    )
    first_mean = jnp.mean(unit_grad, axis=-1, keepdims=True)
    second_mean = jnp.mean(unit_grad * unit_rows, axis=-1, keepdims=True)
    row_grad = (inv_scale * (unit_grad - first_mean - unit_rows * second_mean)).astype(jnp.bfloat16)
    grad_all = lax.all_gather(row_grad, "section", axis=0, tiled=True)
    hidden_grad = 0.5 * lax.dot_general(
        grad_all, down_weight, (((1,), (1,)), ((), ())), preferred_element_type=jnp.float32
    )
    gate_sigmoid = jax.nn.sigmoid(pre_hidden)
    pre_grad = (hidden_grad * gate_sigmoid * (1.0 + pre_hidden * (1.0 - gate_sigmoid))).astype(
        jnp.bfloat16
    )
    up_part = lax.dot_general(
        gathered, pre_grad, (((0,), (0,)), ((), ())), preferred_element_type=jnp.float32
    )
    down_part = 0.5 * lax.dot_general(
        hidden, grad_all, (((0,), (0,)), ((), ())), preferred_element_type=jnp.float32
    )
    weight_parts = jnp.concatenate([up_part, down_part.T], axis=1).astype(jnp.bfloat16)
    weight_pieces = lax.all_to_all(weight_parts, "joint", 0, 0, tiled=True)
    weight_sums = jnp.sum(
        weight_pieces.reshape(joint_count, -1, weight_parts.shape[1]).astype(jnp.float32), axis=0
    )
    hidden_here = up_part.shape[1]
    up_sum = weight_sums[:, :hidden_here]
    down_sum = weight_sums[:, hidden_here:].T
    pred_pieces = jnp.swapaxes(pred_part.reshape(places, section_count, -1), 0, 1)
    pred_sum = jnp.sum(lax.all_to_all(pred_pieces, "section", 0, 0, tiled=True), axis=0)[None]
    return (row_grad[None], up_sum, down_sum, pred_sum)


def solution(mesh):
    return jax.shard_map(
        on_device,
        mesh=mesh,
        in_specs=(
            P("joint", "section", None),
            P(None, "section"),
            P("section", None),
            P(),
            P("joint", None),
            P(),
            P(),
            P(),
            P(),
            P(),
            P(),
            P(),
            P(),
        ),
        out_specs=(
            P("joint", "section", None),
            P("joint", "section"),
            P("section", "joint"),
            P("joint", None, "section"),
        ),
        check_vma=False,
    )
```
